256 devices in a mesh: walker: 2 (over core), grp: 128 (over z, x, y).
Axes of the slice: x: 4, y: 4, z: 8, core: 2. Of those that a mesh axis runs over, the one named last changes fastest.
Arguments:
- feats: bfloat16 [4096, 256], P(('walker', 'grp')), parts along dimension 0, may hold values from -6 to 6
- perm: int32 [4096], P('walker'), parts along dimension 0, may hold values from 0 to 2047, each once
- w_left: bfloat16 [256, 256], replicated, may hold values from -0.375 to 0.375
- w_right: bfloat16 [256, 256], replicated, may hold values from -0.375 to 0.375
- bias_in: float32 [256], replicated, may hold values from -3 to 3
- w_hidden: bfloat16 [256, 256], replicated, may hold values from -0.375 to 0.375
- bias_hidden: float32 [256], replicated, may hold values from -3 to 3
- w_out: float32 [256], replicated, may hold values from -0.375 to 0.375
- pair_strength: float32 [128], replicated, may hold values from 16 to 32
Outputs:
- log_pivot: float32 [256], P('walker'), parts along dimension 0
- panel_cols: float32 [3584, 256], P(('walker', 'grp')), parts along dimension 0
- schur: float32 [3584, 1792], P(('walker', 'grp')), parts along dimension 0
The draws below stay inside these ranges and needn't reach their ends.
There are 2 independent parts, one for each index of `walker`. The reference program is written for one: setup_inputs(seed, part) draws one part's arguments, and reference() takes and returns one part's arrays. A program takes and returns all parts, laid end to end along the dimension named above; an argument that names none is the same for every part. Nothing has to cross between parts.
Inputs may be any that keep to these rules, and one draw needn't show every extreme that they name: `perm`: each position 0 to 2047 appears exactly once.
All inputs are finite; a program needn't handle non-finite values.
Results may differ from the reference program's by a relative error of at most 0.0062.
Values may be sent and summed in bfloat16 or wider, within the bound.
No kernel may reach another device: no remote copies, remote signals or barrier semaphores. Data moves between devices by JAX's collectives and lax.ppermute only.
A program may use at most 64 MiB of HBM per device.

```python
import math
import jax
import jax.numpy as jnp
from jax import lax

NE = 2048
F = 256
H = 256
PANEL = 256
NP = 128


def levels(own_key, dims, shards, low, largest):
    def one(dim, blocks):
        heights = jax.random.uniform(jax.random.fold_in(jax.random.fold_in(own_key, 6), dim), (blocks,), jnp.float32, low / len(shards), largest / len(shards))
        return jnp.repeat(jnp.exp(heights), dims[dim] // blocks).reshape((-1,) + (1,) * (len(dims) - dim - 1))

    gain = one(*shards[0])
    for cut in shards[1:]:
        gain = gain * one(*cut)
    return gain


def noise(stream_key, dims, spread, limit, cuts=(), kind=jnp.bfloat16):
    drawn = jax.random.normal(stream_key, dims, jnp.float32) * spread
    if len(cuts) > 0:
        drawn = levels(stream_key, dims, cuts, -0.22, 0.18) * drawn
    return jnp.clip(drawn, min=-limit, max=limit).astype(kind)


def setup_inputs(seed: int = 0, part: int = 0) -> dict:
    key_of = jax.random.split(jax.random.key(seed), 10)
    part_keys = jax.random.split(jax.random.fold_in(key_of[9], part), 10)
    return {
        "feats": noise(part_keys[0], (NE, F), 1.0, 6.0, ((0, 128),)),
        "perm": jax.random.permutation(part_keys[1], NE).astype(jnp.int32),
        "w_left": noise(key_of[2], (F, H), F ** -0.5, 0.375),
        "w_right": noise(key_of[3], (F, H), F ** -0.5, 0.375),
        "bias_in": noise(key_of[4], (H,), 0.5, 3.0, (), jnp.float32),
        "w_hidden": noise(key_of[5], (H, H), H ** -0.5, 0.375),
        "bias_hidden": noise(key_of[6], (H,), 0.5, 3.0, (), jnp.float32),
        "w_out": noise(key_of[7], (H,), H ** -0.5, 0.375, (), jnp.float32),
        "pair_strength": jnp.clip(jnp.exp(jax.random.uniform(key_of[8], (NP,), jnp.float32, math.log(16.0), math.log(32.0))), 16.0, 32.0),
    }


def orbitals(left_part, right_part, bias_in, w_hidden, bias_hidden, w_out):
    pre = left_part.astype(jnp.float32)[:, None, :] + right_part.astype(jnp.float32)[None, :, :] + bias_in
    gated = jax.nn.silu(pre).astype(jnp.bfloat16).reshape(-1, pre.shape[-1])
    hidden = jax.nn.silu(jnp.dot(gated.astype(jnp.float32), w_hidden.astype(jnp.float32), preferred_element_type=jnp.float32) + bias_hidden)
    values = jnp.dot(hidden, w_out, precision=lax.Precision.HIGHEST)
    return values.reshape(left_part.shape[0], right_part.shape[0])

def factor_block(block):
    size = block.shape[0]
    position = jnp.arange(size).astype(jnp.int32)

    def advance(step, carry):
        matrix, lower, pivots = carry
        first = (2 * step).astype(jnp.int32)
        col_even = lax.dynamic_slice_in_dim(matrix, first, 1, 1)[:, 0]
        col_odd = lax.dynamic_slice_in_dim(matrix, first + 1, 1, 1)[:, 0]
        pivot = lax.dynamic_index_in_dim(col_odd, first, 0, keepdims=False)
        keep = position >= first
        zeros = jnp.zeros_like(col_even)
        lower_even = jnp.where(keep, col_odd / pivot, zeros)
        lower_odd = jnp.where(keep, -col_even / pivot, zeros)
        lower = lax.dynamic_update_slice(lower, jnp.stack([lower_even, lower_odd], axis=1), (jnp.int32(0), first))
        rest = position > first + 1
        keep_even = jnp.where(rest, col_even, zeros)
        keep_odd = jnp.where(rest, col_odd, zeros)
        matrix = matrix + (keep_odd[:, None] * keep_even[None, :] - keep_even[:, None] * keep_odd[None, :]) / pivot
        pivots = lax.dynamic_update_slice(pivots, pivot[None], (step.astype(jnp.int32),))
        return (matrix, lower, pivots)
    start = (block, jnp.zeros_like(block), jnp.zeros((size // 2,), block.dtype))
    matrix, lower, pivots = lax.fori_loop(0, size // 2, advance, start)
    return (lower, pivots)

def pair_scale(columns, pivots):
    count = columns.shape[0]
    grouped = columns.reshape(count, -1, 2)
    swapped = jnp.stack([grouped[:, :, 1], -grouped[:, :, 0]], axis=2).reshape(count, -1)
    return swapped / jnp.repeat(pivots, 2)[None, :]

def reference(feats, perm, w_left, w_right, bias_in, w_hidden, bias_hidden, w_out, pair_strength):
    ordered = jnp.take(feats, perm, axis=0)
    left_all = jnp.dot(ordered.astype(jnp.float32), w_left.astype(jnp.float32), preferred_element_type=jnp.float32).astype(jnp.bfloat16)
    right_all = jnp.dot(ordered.astype(jnp.float32), w_right.astype(jnp.float32), preferred_element_type=jnp.float32).astype(jnp.bfloat16)
    stacked = left_all.reshape(NE // 16, 16, H)
    orbital = lax.map(lambda piece: orbitals(piece, right_all, bias_in, w_hidden, bias_hidden, w_out), stacked)
    orbital = orbital.reshape(NE, NE)
    pattern = jnp.array([[0.0, 1.0], [-1.0, 0.0]], dtype=pair_strength.dtype)
    block = orbital[:PANEL, :PANEL] - orbital[:PANEL, :PANEL].T + jnp.kron(jnp.diag(pair_strength), pattern)
    below = orbital[PANEL:, :PANEL] - orbital[:PANEL, PANEL:].T
    trailing = orbital[PANEL:, PANEL:] - orbital[PANEL:, PANEL:].T
    lower, pivots = factor_block(block)
    log_pivot = jnp.log(jnp.abs(pivots))
    panel_cols = jax.scipy.linalg.solve_triangular(lower, below.T, lower=True, unit_diagonal=True).T
    scaled = pair_scale(panel_cols, pivots)
    schur = trailing - jnp.dot(panel_cols, scaled.T, precision=lax.Precision.HIGHEST)
    return (log_pivot, panel_cols, schur)
```

```python
import jax
import jax.numpy as jnp
from jax import lax
from jax.experimental import pallas as pl
from jax.experimental.pallas import tpu as pltpu
from jax.sharding import PartitionSpec as P


def orbitals(left_part, right_part, bias_in, w_hidden, bias_hidden, w_out):
    pre = (
        left_part.astype(jnp.float32)[:, None, :]
        + right_part.astype(jnp.float32)[None, :, :]
        + bias_in
    )
    gated = jax.nn.silu(pre).astype(jnp.bfloat16).reshape(-1, pre.shape[-1])
    hidden = jax.nn.silu(jnp.dot(gated, w_hidden, preferred_element_type=jnp.float32) + bias_hidden)
    values = jnp.dot(hidden, w_out, precision=lax.Precision.HIGHEST)
    return values.reshape(left_part.shape[0], right_part.shape[0])


def column_width():
    return 128


def forward_terms(left_rows, right_cols, params):
    count = right_cols.shape[0]
    width = column_width()
    pieces = right_cols.reshape(count // width, width, right_cols.shape[1])
    result = lax.map(lambda piece: orbitals(left_rows, piece, *params), pieces)
    return jnp.transpose(result, (1, 0, 2)).reshape(left_rows.shape[0], count)


def backward_terms(right_rows, left_cols, params):
    count = left_cols.shape[0]
    width = column_width()
    pieces = left_cols.reshape(count // width, width, left_cols.shape[1])
    result = lax.map(lambda piece: orbitals(piece, right_rows, *params), pieces)
    return result.reshape(count, right_rows.shape[0]).T


def factor_kernel(m_in_ref, m_ref):
    m_ref[...] = m_in_ref[...]
    rows, size = m_ref.shape
    lane = lax.broadcasted_iota(jnp.int32, (1, size), 1)
    lanes = lax.broadcasted_iota(jnp.int32, (rows, size), 1)
    row_idx = lax.broadcasted_iota(jnp.int32, (rows, 1), 0)

    def step(k, carry):
        first = 2 * k
        r0 = m_ref[pl.ds(first, 1), :]
        r1 = m_ref[pl.ds(first + 1, 1), :]
        pivot = jnp.sum(jnp.where(lane == first + 1, r0, 0.0), axis=1, keepdims=True)
        keep_lane = lane > first + 1
        even_lane = jnp.where(keep_lane, -r0 / pivot, 0.0)
        odd_lane = jnp.where(keep_lane, -r1 / pivot, 0.0)
        m = m_ref[...]
        col_even = jnp.sum(jnp.where(lanes == first, m, 0.0), axis=1, keepdims=True)
        col_odd = jnp.sum(jnp.where(lanes == first + 1, m, 0.0), axis=1, keepdims=True)
        keep_row = row_idx > first + 1
        col_even = jnp.where(keep_row, col_even, 0.0)
        col_odd = jnp.where(keep_row, col_odd, 0.0)
        m_ref[...] = m + (col_odd * even_lane - col_even * odd_lane)
        return carry

    lax.fori_loop(0, size // 2, step, 0)


def factor_augmented(matrix):
    return pl.pallas_call(
        factor_kernel,
        out_shape=jax.ShapeDtypeStruct(matrix.shape, matrix.dtype),
        in_specs=[pl.BlockSpec(memory_space=pltpu.VMEM)],
        out_specs=pl.BlockSpec(memory_space=pltpu.VMEM),
    )(matrix)


def pair_scale(columns, pivots):
    count = columns.shape[0]
    grouped = columns.reshape(count, -1, 2)
    swapped = jnp.stack([grouped[:, :, 1], -grouped[:, :, 0]], axis=2).reshape(count, -1)
    return swapped / jnp.repeat(pivots, 2)[None, :]


def on_device(feats, perm, w_left, w_right, bias_in, w_hidden, bias_hidden, w_out, pair_strength):
    groups = lax.axis_size("grp")
    device = lax.axis_index("grp")
    electrons = perm.shape[0]
    hid = w_left.shape[1]
    panel = 2 * pair_strength.shape[0]
    share = panel // groups
    tail = (electrons - panel) // groups
    params = (bias_in, w_hidden, bias_hidden, w_out)
    w_both = jnp.concatenate([w_left, w_right], axis=1)
    both_own = jnp.dot(feats, w_both, preferred_element_type=jnp.float32).astype(jnp.bfloat16)
    both_every = lax.all_gather(both_own, "grp", axis=0, tiled=True)
    both_all = jnp.take(both_every, perm, axis=0)
    left_all = both_all[:, :hid]
    right_all = both_all[:, hid:]
    top_start = device * share
    tail_start = panel + device * tail
    left_top = lax.dynamic_slice_in_dim(left_all, top_start, share, 0)
    right_top = lax.dynamic_slice_in_dim(right_all, top_start, share, 0)
    left_tail = lax.dynamic_slice_in_dim(left_all, tail_start, tail, 0)
    right_tail = lax.dynamic_slice_in_dim(right_all, tail_start, tail, 0)
    top_rows = forward_terms(left_top, right_all[:panel], params) - backward_terms(
        right_top, left_all[:panel], params
    )
    pad = (-share) % 8
    top_padded = jnp.pad(top_rows, ((0, pad), (0, 0)))
    gathered = lax.all_gather(top_padded, "grp", axis=0, tiled=False)
    block_rows = gathered[:, :share, :].reshape(panel, panel)
    tail_rows = forward_terms(left_tail, right_all, params) - backward_terms(
        right_tail, left_all, params
    )
    pattern = jnp.array([[0.0, 1.0], [-1.0, 0.0]], dtype=pair_strength.dtype)
    block = block_rows + jnp.kron(jnp.diag(pair_strength), pattern)
    below_own = tail_rows[:, :panel]
    trailing_own = tail_rows[:, panel:]
    extra = (-tail) % 8
    augmented = jnp.concatenate(
        [block, below_own, jnp.zeros((extra, panel), block.dtype)], axis=0
    )
    factored = factor_augmented(augmented)
    pairs = factored[:panel].reshape(panel // 2, 2, panel // 2, 2)
    pivots = jnp.diagonal(pairs[:, 0, :, 1])
    log_pivot = jnp.log(jnp.abs(pivots))
    panel_own = factored[panel:panel + tail]
    scaled_own = pair_scale(panel_own, pivots)
    schur = trailing_own - jnp.dot(
        panel_own,
        lax.all_gather(scaled_own, "grp", axis=0, tiled=True).T,
        precision=lax.Precision.HIGHEST,
    )
    return (log_pivot, panel_own, schur)


def solution(mesh):
    return jax.shard_map(
        on_device,
        mesh=mesh,
        in_specs=(P(("walker", "grp"), None), P("walker"), P(), P(), P(), P(), P(), P(), P()),
        out_specs=(P("walker"), P(("walker", "grp"), None), P(("walker", "grp"), None)),
        check_vma=False,
    )
```

```python
import numpy as np
import jax
import jax.numpy as jnp
from jax import lax
from jax.experimental import pallas as pl
from jax.experimental.pallas import tpu as pltpu
from jax.sharding import Mesh
from jax.sharding import PartitionSpec as P


def silu(v):
    half = 0.5 * v
    return half * (1.0 + jnp.tanh(half))


def orbital_kernel(col_ref, mat_ref, bias_in_ref, w_hid_t_ref, bias_hid_ref, w_out_ref, out_ref):
    rows = col_ref.shape[1]
    bias_in = bias_in_ref[...]
    bias_hid = bias_hid_ref[...]
    w_out = w_out_ref[...]
    w_hid_t = w_hid_t_ref[...]

    def one(d, r):
        pre = (col_ref[d, r] + mat_ref[d]) + bias_in
        gated = silu(pre).astype(jnp.bfloat16)
        hidden = jnp.dot(w_hid_t, gated, preferred_element_type=jnp.float32)
        hidden = silu(hidden + bias_hid)
        return jnp.sum(hidden * w_out, axis=0, keepdims=True)

    def body(r, carry):
        out_ref[pl.ds(r, 1), :] = one(0, r) - one(1, r)
        return carry

    lax.fori_loop(0, rows, body, 0)


def orbital_rows(cols, mats, bias_in, w_hid_t, bias_hid, w_out):
    _, rows, feat, _ = cols.shape
    count = mats.shape[2]
    width = min(count, 256)
    flops = 2 * rows * count * (2 * feat * feat + 12 * feat)
    return pl.pallas_call(
        orbital_kernel,
        grid=(count // width,),
        out_shape=jax.ShapeDtypeStruct((rows, count), jnp.float32),
        in_specs=[
            pl.BlockSpec((2, rows, feat, 1), lambda j: (0, 0, 0, 0)),
            pl.BlockSpec((2, feat, width), lambda j: (0, 0, j)),
            pl.BlockSpec((feat, 1), lambda j: (0, 0)),
            pl.BlockSpec((feat, feat), lambda j: (0, 0)),
            pl.BlockSpec((feat, 1), lambda j: (0, 0)),
            pl.BlockSpec((feat, 1), lambda j: (0, 0)),
        ],
        out_specs=pl.BlockSpec((rows, width), lambda j: (0, j)),
        cost_estimate=pl.CostEstimate(
            flops=flops,
            transcendentals=4 * rows * count * feat,
            bytes_accessed=4 * (2 * feat * count + rows * count),
        ),
    )(cols, mats, bias_in, w_hid_t, bias_hid, w_out)


def factor_kernel(m_in_ref, ps_ref, pc_ref, piv_ref, scaled_ref, m_ref):
    rows, size = m_ref.shape
    lane = lax.broadcasted_iota(jnp.int32, (1, size), 1)
    lanes = lax.broadcasted_iota(jnp.int32, (rows, size), 1)
    row_idx = lax.broadcasted_iota(jnp.int32, (rows, 1), 0)
    m0 = m_in_ref[...]
    strength = ps_ref[...]
    m0 = m0 + jnp.where((row_idx % 2 == 0) & (lanes == row_idx + 1) & (row_idx < size), strength, 0.0)
    m0 = m0 - jnp.where((row_idx % 2 == 1) & (lanes == row_idx - 1) & (row_idx < size), strength, 0.0)
    m_ref[...] = m0
    below = rows - size

    def step(k, carry):
        pivots, scaled = carry
        first = 2 * k
        r0 = m_ref[pl.ds(first, 1), :]
        r1 = m_ref[pl.ds(first + 1, 1), :]
        pivot = jnp.sum(jnp.where(lane == first + 1, r0, 0.0), axis=1, keepdims=True)
        keep_lane = lane > first + 1
        even_lane = jnp.where(keep_lane, -r0 / pivot, 0.0)
        odd_lane = jnp.where(keep_lane, -r1 / pivot, 0.0)
        m = m_ref[...]
        col_even = jnp.sum(jnp.where(lanes == first, m, 0.0), axis=1, keepdims=True)
        col_odd = jnp.sum(jnp.where(lanes == first + 1, m, 0.0), axis=1, keepdims=True)
        low_even = col_even[size:]
        low_odd = col_odd[size:]
        low_lanes = lanes[size:]
        scaled = jnp.where(low_lanes == first, low_odd / pivot, scaled)
        scaled = jnp.where(low_lanes == first + 1, -low_even / pivot, scaled)
        pivots = jnp.where(lane == k, pivot, pivots)
        keep_row = row_idx > first + 1
        col_even = jnp.where(keep_row, col_even, 0.0)
        col_odd = jnp.where(keep_row, col_odd, 0.0)
        m_ref[...] = m + (col_odd * even_lane - col_even * odd_lane)
        return (pivots, scaled)

    start = (jnp.zeros((1, size), jnp.float32), jnp.zeros((below, size), jnp.float32))
    pivots, scaled = lax.fori_loop(0, size // 2, step, start)
    pc_ref[...] = m_ref[size:, :]
    piv_ref[...] = pivots
    scaled_ref[...] = scaled


def factor_augmented(matrix, strength_col, size):
    rows, width = matrix.shape
    below = rows - size
    vmem = pl.BlockSpec(memory_space=pltpu.VMEM)
    return pl.pallas_call(
        factor_kernel,
        out_shape=(
            jax.ShapeDtypeStruct((below, width), jnp.float32),
            jax.ShapeDtypeStruct((1, width), jnp.float32),
            jax.ShapeDtypeStruct((below, width), jnp.float32),
        ),
        in_specs=[vmem, vmem],
        out_specs=(vmem, vmem, vmem),
        scratch_shapes=[pltpu.VMEM((rows, width), jnp.float32)],
    )(matrix, strength_col)


def gather_rows(x, stages):
    for axes in stages:
        x = lax.all_gather(x, axes, axis=0, tiled=True)
    return x


def make_on_device(stages, grp_axes):
    def on_device(feats, perm, w_left, w_right, bias_in, w_hidden, bias_hidden, w_out, pair_strength):
        groups = lax.psum(1, grp_axes)
        device = lax.axis_index(grp_axes)
        electrons = perm.shape[0]
        hid = w_left.shape[1]
        panel = 2 * pair_strength.shape[0]
        share = panel // groups
        tail = (electrons - panel) // groups
        w_both = jnp.concatenate([w_left, w_right], axis=1)
        both_own = jnp.dot(feats, w_both, preferred_element_type=jnp.float32).astype(jnp.bfloat16)
        both_every = gather_rows(both_own, stages)
        both_all = jnp.take(both_every, perm, axis=0).astype(jnp.float32)
        mats = jnp.stack([both_all[:, hid:].T, both_all[:, :hid].T])
        params = (
            bias_in[:, None],
            w_hidden.T,
            bias_hidden[:, None],
            w_out[:, None],
        )
        top_start = device * share
        tail_start = panel + device * tail
        top_own = lax.dynamic_slice_in_dim(both_all, top_start, share, 0)
        tail_own = lax.dynamic_slice_in_dim(both_all, tail_start, tail, 0)
        top_cols = jnp.stack([top_own[:, :hid], top_own[:, hid:]])[..., None]
        tail_cols = jnp.stack([tail_own[:, :hid], tail_own[:, hid:]])[..., None]
        top_rows = orbital_rows(top_cols, mats[:, :, :panel], *params)
        pad = (-share) % 8
        top_padded = jnp.pad(top_rows, ((0, pad), (0, 0)))
        gathered = gather_rows(top_padded, stages)
        block_rows = gathered.reshape(groups, share + pad, panel)[:, :share, :].reshape(panel, panel)
        tail_rows = orbital_rows(tail_cols, mats, *params)
        below_own = tail_rows[:, :panel]
        trailing_own = tail_rows[:, panel:]
        extra = (-tail) % 8
        augmented = jnp.concatenate(
            [block_rows, below_own, jnp.zeros((extra, panel), jnp.float32)], axis=0
        )
        strength_col = jnp.concatenate(
            [jnp.repeat(pair_strength, 2), jnp.zeros((tail + extra,), jnp.float32)]
        )[:, None]
        pc, piv_row, scaled = factor_augmented(augmented, strength_col, panel)
        pivots = piv_row[0, : panel // 2]
        log_pivot = jnp.log(jnp.abs(pivots))
        panel_own = pc[:tail]
        scaled_own = scaled[:tail]
        schur = trailing_own - jnp.dot(
            panel_own,
            gather_rows(scaled_own, stages).T,
            precision=lax.Precision.HIGHEST,
        )
        return (log_pivot, panel_own, schur)

    return on_device


def split_grp(mesh):
    devs = mesh.devices
    try:
        coords = np.array([[d.coords[2], d.coords[0], d.coords[1]] for d in devs[0]])
        sizes = tuple(len(np.unique(coords[:, i])) for i in range(3))
        grid = coords.reshape(sizes + (3,))
        ok = int(np.prod(sizes)) == devs.shape[1]
        for i in range(3):
            idx = np.arange(sizes[i]).reshape([-1 if j == i else 1 for j in range(3)])
            ok = ok and bool(np.all(grid[..., i] == idx))
    except Exception:
        ok = False
    if not ok:
        return None
    return Mesh(devs.reshape((devs.shape[0],) + sizes), ("walker", "z", "x", "y"))


def solution(mesh):
    split = split_grp(mesh)
    if split is None:
        use, grp_axes, stages = mesh, "grp", ("grp",)
    else:
        use, grp_axes, stages = split, ("z", "x", "y"), (("x", "y"), "z")
    rows = ("walker",) + ((grp_axes,) if isinstance(grp_axes, str) else grp_axes)
    return jax.shard_map(
        make_on_device(stages, grp_axes),
        mesh=use,
        in_specs=(P(rows, None), P("walker"), P(), P(), P(), P(), P(), P(), P()),
        out_specs=(P("walker"), P(rows, None), P(rows, None)),
        check_vma=False,
    )
```

```python
import numpy as np
import jax
import jax.numpy as jnp
from jax import lax
from jax.experimental import pallas as pl
from jax.experimental.pallas import tpu as pltpu
from jax.sharding import Mesh
from jax.sharding import PartitionSpec as P


def orbital_kernel(col_ref, mat_ref, bias_in_ref, w_hid_t_ref, bias_hid_ref, w_out_ref, *rest):
    out_ref = rest[-1]
    rows = col_ref.shape[1]
    bias_in = bias_in_ref[...]
    bias_hid = bias_hid_ref[...]
    w_out = w_out_ref[...]
    w_hid_t = w_hid_t_ref[...]

    def one(d, r):
        half = (col_ref[d, r] + mat_ref[d]) + bias_in
        gated = (half * (1.0 + jnp.tanh(half))).astype(jnp.bfloat16)
        half = jnp.dot(w_hid_t, gated, preferred_element_type=jnp.float32) + bias_hid
        return jnp.sum(half * (1.0 + jnp.tanh(half)) * w_out, axis=0, keepdims=True)

    def body(r, carry):
        out_ref[pl.ds(r, 1), :] = one(0, r) - one(1, r)
        return carry

    lax.fori_loop(0, rows, body, 0)


def orbital_rows(cols, mats, params, first, blocks, width, after=None):
    _, rows, feat, _ = cols.shape
    count = blocks * width
    flops = 2 * rows * count * (2 * feat * feat + 12 * feat)
    operands = [cols, mats, *params]
    in_specs = [
        pl.BlockSpec((2, rows, feat, 1), lambda j: (0, 0, 0, 0)),
        pl.BlockSpec((2, feat, width), lambda j: (0, 0, j + first)),
        pl.BlockSpec((feat, 1), lambda j: (0, 0)),
        pl.BlockSpec((feat, feat), lambda j: (0, 0)),
        pl.BlockSpec((feat, 1), lambda j: (0, 0)),
        pl.BlockSpec((feat, 1), lambda j: (0, 0)),
    ]
    if after is not None:
        operands.append(after)
        in_specs.append(pl.BlockSpec(after.shape, lambda j: (0, 0)))
    return pl.pallas_call(
        orbital_kernel,
        grid=(blocks,),
        out_shape=jax.ShapeDtypeStruct((rows, count), jnp.float32),
        in_specs=in_specs,
        out_specs=pl.BlockSpec((rows, width), lambda j: (0, j)),
        cost_estimate=pl.CostEstimate(
            flops=flops,
            transcendentals=4 * rows * count * feat,
            bytes_accessed=4 * (2 * feat * count + rows * count),
        ),
    )(*operands)


def factor_kernel(m_in_ref, ps_ref, after_ref, pc_ref, piv_ref, scaled_ref, m_ref):
    rows, size = m_ref.shape
    lane = lax.broadcasted_iota(jnp.int32, (1, size), 1)
    lanes = lax.broadcasted_iota(jnp.int32, (rows, size), 1)
    row_idx = lax.broadcasted_iota(jnp.int32, (rows, 1), 0)
    m0 = m_in_ref[...]
    strength = ps_ref[...]
    m0 = m0 + jnp.where((row_idx % 2 == 0) & (lanes == row_idx + 1) & (row_idx < size), strength, 0.0)
    m0 = m0 - jnp.where((row_idx % 2 == 1) & (lanes == row_idx - 1) & (row_idx < size), strength, 0.0)
    m_ref[...] = m0
    below = rows - size

    def step(k, carry):
        pivots, scaled = carry
        first = 2 * k
        r0 = m_ref[pl.ds(first, 1), :]
        r1 = m_ref[pl.ds(first + 1, 1), :]
        pivot = jnp.sum(jnp.where(lane == first + 1, r0, 0.0), axis=1, keepdims=True)
        keep_lane = lane > first + 1
        even_lane = jnp.where(keep_lane, -r0 / pivot, 0.0)
        odd_lane = jnp.where(keep_lane, -r1 / pivot, 0.0)
        m = m_ref[...]
        col_even = jnp.sum(jnp.where(lanes == first, m, 0.0), axis=1, keepdims=True)
        col_odd = jnp.sum(jnp.where(lanes == first + 1, m, 0.0), axis=1, keepdims=True)
        low_even = col_even[size:]
        low_odd = col_odd[size:]
        low_lanes = lanes[size:]
        scaled = jnp.where(low_lanes == first, low_odd / pivot, scaled)
        scaled = jnp.where(low_lanes == first + 1, -low_even / pivot, scaled)
        pivots = jnp.where(lane == k, pivot, pivots)
        keep_row = row_idx > first + 1
        col_even = jnp.where(keep_row, col_even, 0.0)
        col_odd = jnp.where(keep_row, col_odd, 0.0)
        m_ref[...] = m + (col_odd * even_lane - col_even * odd_lane)
        return (pivots, scaled)

    start = (jnp.zeros((1, size), jnp.float32), jnp.zeros((below, size), jnp.float32))
    pivots, scaled = lax.fori_loop(0, size // 2, step, start)
    pc_ref[...] = m_ref[size:, :]
    piv_ref[...] = pivots
    scaled_ref[...] = scaled


def factor_augmented(matrix, strength_col, size, after):
    rows, width = matrix.shape
    below = rows - size
    vmem = pl.BlockSpec(memory_space=pltpu.VMEM)
    return pl.pallas_call(
        factor_kernel,
        out_shape=(
            jax.ShapeDtypeStruct((below, width), jnp.float32),
            jax.ShapeDtypeStruct((1, width), jnp.float32),
            jax.ShapeDtypeStruct((below, width), jnp.float32),
        ),
        in_specs=[vmem, vmem, vmem],
        out_specs=(vmem, vmem, vmem),
        scratch_shapes=[pltpu.VMEM((rows, width), jnp.float32)],
    )(matrix, strength_col, after)


def gather_rows(x, stages):
    for axes in stages:
        x = lax.all_gather(x, axes, axis=0, tiled=True)
    return x


def make_on_device(stages, grp_axes):
    def on_device(feats, perm, w_left, w_right, bias_in, w_hidden, bias_hidden, w_out, pair_strength):
        groups = lax.psum(1, grp_axes)
        device = lax.axis_index(grp_axes)
        electrons = perm.shape[0]
        hid = w_left.shape[1]
        panel = 2 * pair_strength.shape[0]
        share = panel // groups
        tail = (electrons - panel) // groups
        w_both = jnp.concatenate([w_left, w_right], axis=1)
        both_own = jnp.dot(feats, w_both, preferred_element_type=jnp.float32).astype(jnp.bfloat16)
        both_every = gather_rows(both_own, stages)
        both_all = jnp.take(both_every, perm, axis=0).astype(jnp.float32)
        halves = 0.5 * both_all
        mats = jnp.stack([halves[:, hid:].T, halves[:, :hid].T])
        params = (
            0.5 * bias_in[:, None],
            (w_hidden.T * 0.5).astype(w_hidden.dtype),
            0.5 * bias_hidden[:, None],
            w_out[:, None],
        )
        width = panel
        top_start = device * share
        tail_start = panel + device * tail
        top_own = lax.dynamic_slice_in_dim(halves, top_start, share, 0)
        tail_own = lax.dynamic_slice_in_dim(halves, tail_start, tail, 0)
        top_cols = jnp.stack([top_own[:, :hid], top_own[:, hid:]])[..., None]
        tail_cols = jnp.stack([tail_own[:, :hid], tail_own[:, hid:]])[..., None]
        top_rows = orbital_rows(top_cols, mats, params, 0, 1, width)
        pad = (-share) % 8
        top_padded = jnp.pad(top_rows, ((0, pad), (0, 0)))
        gathered = gather_rows(top_padded, stages)
        block_rows = gathered.reshape(groups, share + pad, panel)[:, :share, :].reshape(panel, panel)
        blocks = electrons // width
        early = (blocks - 1) // 2
        below_own = orbital_rows(tail_cols, mats, params, 0, 1, width)
        trailing_a = orbital_rows(tail_cols, mats, params, 1, early, width)
        extra = (-tail) % 8
        augmented = jnp.concatenate(
            [block_rows, below_own, jnp.zeros((extra, panel), jnp.float32)], axis=0
        )
        strength_col = jnp.concatenate(
            [jnp.repeat(pair_strength, 2), jnp.zeros((tail + extra,), jnp.float32)]
        )[:, None]
        pc, piv_row, scaled = factor_augmented(augmented, strength_col, panel, trailing_a[:8, :128])
        pivots = piv_row[0, : panel // 2]
        log_pivot = jnp.log(jnp.abs(pivots))
        panel_own = pc[:tail]
        scaled_own = scaled[:tail]
        scaled_all = gather_rows(scaled_own, stages)
        trailing_b = orbital_rows(
            tail_cols, mats, params, 1 + early, blocks - 1 - early, width, after=piv_row
        )
        trailing_own = jnp.concatenate([trailing_a, trailing_b], axis=1)
        schur = trailing_own - jnp.dot(
            panel_own,
            scaled_all.T,
            precision=lax.Precision.HIGHEST,
        )
        return (log_pivot, panel_own, schur)

    return on_device


def split_grp(mesh):
    devs = mesh.devices
    try:
        coords = np.array([[d.coords[2], d.coords[0], d.coords[1]] for d in devs[0]])
        sizes = tuple(len(np.unique(coords[:, i])) for i in range(3))
        grid = coords.reshape(sizes + (3,))
        ok = int(np.prod(sizes)) == devs.shape[1]
        for i in range(3):
            idx = np.arange(sizes[i]).reshape([-1 if j == i else 1 for j in range(3)])
            ok = ok and bool(np.all(grid[..., i] == idx))
    except Exception:
        ok = False
    if not ok:
        return None
    return Mesh(devs.reshape((devs.shape[0],) + sizes), ("walker", "z", "x", "y"))


def solution(mesh):
    split = split_grp(mesh)
    if split is None:
        use, grp_axes, stages = mesh, "grp", ("grp",)
    else:
        use, grp_axes, stages = split, ("z", "x", "y"), (("x", "y"), "z")
    rows = ("walker",) + ((grp_axes,) if isinstance(grp_axes, str) else grp_axes)
    return jax.shard_map(
        make_on_device(stages, grp_axes),
        mesh=use,
        in_specs=(P(rows, None), P("walker"), P(), P(), P(), P(), P(), P(), P()),
        out_specs=(P("walker"), P(rows, None), P(rows, None)),
        check_vma=False,
    )
```

```python
import numpy as np
import jax
import jax.numpy as jnp
from jax import lax
from jax.experimental import pallas as pl
from jax.experimental.pallas import tpu as pltpu
from jax.sharding import Mesh
from jax.sharding import PartitionSpec as P


def orbital_kernel(col_ref, mat_ref, bias_in_ref, w_hid_t_ref, bias_hid_ref, w_out_ref, *rest):
    out_ref = rest[-1]
    rows = col_ref.shape[1]
    copies = mat_ref.shape[2] // col_ref.shape[3]
    w_hid_t = w_hid_t_ref[...]

    def one(d, r):
        col = col_ref[d, r]
        col = jnp.concatenate([col] * copies, axis=1) if copies > 1 else col
        half = (col + mat_ref[d]) + bias_in_ref[...]
        gated = (half * (1.0 + jnp.tanh(half))).astype(jnp.bfloat16)
        half = jnp.dot(w_hid_t, gated, preferred_element_type=jnp.float32) + bias_hid_ref[...]
        return jnp.sum(half * (1.0 + jnp.tanh(half)) * w_out_ref[...], axis=0, keepdims=True)

    def body(r, carry):
        out_ref[pl.ds(r, 1), :] = one(0, r) - one(1, r)
        return carry

    lax.fori_loop(0, rows, body, 0)


def orbital_rows(cols, mats, params, first, blocks, width, after=None):
    _, rows, feat, lanes = cols.shape
    count = blocks * width
    flops = 2 * rows * count * (2 * feat * feat + 12 * feat)
    operands = [cols, mats, *params]
    in_specs = [
        pl.BlockSpec((2, rows, feat, lanes), lambda j: (0, 0, 0, 0)),
        pl.BlockSpec((2, feat, width), lambda j: (0, 0, j + first)),
        pl.BlockSpec((feat, width), lambda j: (0, 0)),
        pl.BlockSpec((feat, feat), lambda j: (0, 0)),
        pl.BlockSpec((feat, width), lambda j: (0, 0)),
        pl.BlockSpec((feat, width), lambda j: (0, 0)),
    ]
    if after is not None:
        operands.append(after)
        in_specs.append(pl.BlockSpec(after.shape, lambda j: (0, 0)))
    return pl.pallas_call(
        orbital_kernel,
        grid=(blocks,),
        out_shape=jax.ShapeDtypeStruct((rows, count), jnp.float32),
        in_specs=in_specs,
        out_specs=pl.BlockSpec((rows, width), lambda j: (0, j)),
        cost_estimate=pl.CostEstimate(
            flops=flops,
            transcendentals=4 * rows * count * feat,
            bytes_accessed=4 * (2 * feat * count + rows * count),
        ),
    )(*operands)


def factor_kernel(m_in_ref, ps_ref, after_ref, pc_ref, piv_ref, scaled_ref, m_ref):
    rows, size = m_ref.shape
    lane = lax.broadcasted_iota(jnp.int32, (1, size), 1)
    lanes = lax.broadcasted_iota(jnp.int32, (rows, size), 1)
    row_idx = lax.broadcasted_iota(jnp.int32, (rows, 1), 0)
    m0 = m_in_ref[...]
    strength = ps_ref[...]
    m0 = m0 + jnp.where((row_idx % 2 == 0) & (lanes == row_idx + 1) & (row_idx < size), strength, 0.0)
    m0 = m0 - jnp.where((row_idx % 2 == 1) & (lanes == row_idx - 1) & (row_idx < size), strength, 0.0)
    m_ref[...] = m0
    below = rows - size

    def step(k, carry):
        pivots, scaled = carry
        first = 2 * k
        r0 = m_ref[pl.ds(first, 1), :]
        r1 = m_ref[pl.ds(first + 1, 1), :]
        pivot = jnp.sum(jnp.where(lane == first + 1, r0, 0.0), axis=1, keepdims=True)
        keep_lane = lane > first + 1
        even_lane = jnp.where(keep_lane, -r0 / pivot, 0.0)
        odd_lane = jnp.where(keep_lane, -r1 / pivot, 0.0)
        m = m_ref[...]
        col_even = jnp.sum(jnp.where(lanes == first, m, 0.0), axis=1, keepdims=True)
        col_odd = jnp.sum(jnp.where(lanes == first + 1, m, 0.0), axis=1, keepdims=True)
        low_even = col_even[size:]
        low_odd = col_odd[size:]
        low_lanes = lanes[size:]
        scaled = jnp.where(low_lanes == first, low_odd / pivot, scaled)
        scaled = jnp.where(low_lanes == first + 1, -low_even / pivot, scaled)
        pivots = jnp.where(lane == k, pivot, pivots)
        keep_row = row_idx > first + 1
        col_even = jnp.where(keep_row, col_even, 0.0)
        col_odd = jnp.where(keep_row, col_odd, 0.0)
        m_ref[...] = m + (col_odd * even_lane - col_even * odd_lane)
        return (pivots, scaled)

    start = (jnp.zeros((1, size), jnp.float32), jnp.zeros((below, size), jnp.float32))
    pivots, scaled = lax.fori_loop(0, size // 2, step, start)
    pc_ref[...] = m_ref[size:, :]
    piv_ref[...] = pivots
    scaled_ref[...] = scaled


def factor_augmented(matrix, strength_col, size, after):
    rows, width = matrix.shape
    below = rows - size
    vmem = pl.BlockSpec(memory_space=pltpu.VMEM)
    return pl.pallas_call(
        factor_kernel,
        out_shape=(
            jax.ShapeDtypeStruct((below, width), jnp.float32),
            jax.ShapeDtypeStruct((1, width), jnp.float32),
            jax.ShapeDtypeStruct((below, width), jnp.float32),
        ),
        in_specs=[vmem, vmem, vmem],
        out_specs=(vmem, vmem, vmem),
        scratch_shapes=[pltpu.VMEM((rows, width), jnp.float32)],
    )(matrix, strength_col, after)


def gather_rows(x, stages):
    return gather_stages(x, stages)[-1]


def gather_stages(x, stages):
    outs = []
    for axes in stages:
        x = lax.all_gather(x, axes, axis=0, tiled=True)
        outs.append(x)
    return outs


def make_on_device(stages, grp_axes):
    def on_device(feats, perm, w_left, w_right, bias_in, w_hidden, bias_hidden, w_out, pair_strength):
        groups = lax.psum(1, grp_axes)
        device = lax.axis_index(grp_axes)
        electrons = perm.shape[0]
        hid = w_left.shape[1]
        panel = 2 * pair_strength.shape[0]
        share = panel // groups
        tail = (electrons - panel) // groups
        w_both = jnp.concatenate([w_left, w_right], axis=1)
        both_own = jnp.dot(feats, w_both, preferred_element_type=jnp.float32).astype(jnp.bfloat16)
        both_every = gather_rows(both_own, stages)
        width = panel
        lanes = 128

        def columns(rows_both):
            stacked = jnp.stack([rows_both[:, :hid], rows_both[:, hid:]])[..., None]
            return jnp.broadcast_to(stacked, stacked.shape[:-1] + (lanes,))

        def transposed(rows_both):
            return jnp.stack([rows_both[:, hid:].T, rows_both[:, :hid].T])

        params = (
            jnp.broadcast_to(0.5 * bias_in[:, None], (hid, width)),
            (w_hidden.T * 0.5).astype(w_hidden.dtype),
            jnp.broadcast_to(0.5 * bias_hidden[:, None], (hid, width)),
            jnp.broadcast_to(w_out[:, None], (hid, width)),
        )
        top_both = 0.5 * jnp.take(both_every, perm[:panel], axis=0).astype(jnp.float32)
        top_own = lax.dynamic_slice_in_dim(top_both, device * share, share, 0)
        top_rows = orbital_rows(columns(top_own), transposed(top_both), params, 0, 1, width)
        pad = (-share) % 8
        top_padded = jnp.pad(top_rows, ((0, pad), (0, 0)))
        partial = gather_stages(top_padded, stages)
        gathered = partial[-1]
        late_every, _ = lax.optimization_barrier((both_every, partial[0]))
        halves = 0.5 * jnp.take(late_every, perm, axis=0).astype(jnp.float32)
        mats = transposed(halves)
        tail_own = lax.dynamic_slice_in_dim(halves, panel + device * tail, tail, 0)
        tail_cols = columns(tail_own)
        block_rows = gathered.reshape(groups, share + pad, panel)[:, :share, :].reshape(panel, panel)
        blocks = electrons // width
        early = (blocks - 1) // 2
        below_own = orbital_rows(tail_cols, mats, params, 0, 1, width)
        trailing_a = orbital_rows(tail_cols, mats, params, 1, early, width)
        extra = (-tail) % 8
        augmented = jnp.concatenate(
            [block_rows, below_own, jnp.zeros((extra, panel), jnp.float32)], axis=0
        )
        strength_col = jnp.concatenate(
            [jnp.repeat(pair_strength, 2), jnp.zeros((tail + extra,), jnp.float32)]
        )[:, None]
        pc, piv_row, scaled = factor_augmented(augmented, strength_col, panel, trailing_a[:8, :128])
        pivots = piv_row[0, : panel // 2]
        log_pivot = jnp.log(jnp.abs(pivots))
        panel_own = pc[:tail]
        scaled_own = scaled[:tail]
        scaled_all = gather_rows(scaled_own, stages)
        trailing_b = orbital_rows(
            tail_cols, mats, params, 1 + early, blocks - 1 - early, width, after=piv_row
        )
        trailing_own = jnp.concatenate([trailing_a, trailing_b], axis=1)
        schur = trailing_own - jnp.dot(
            panel_own,
            scaled_all.T,
            precision=lax.Precision.HIGHEST,
        )
        return (log_pivot, panel_own, schur)

    return on_device


def split_grp(mesh):
    devs = mesh.devices
    try:
        coords = np.array([[d.coords[2], d.coords[0], d.coords[1]] for d in devs[0]])
        sizes = tuple(len(np.unique(coords[:, i])) for i in range(3))
        grid = coords.reshape(sizes + (3,))
        ok = int(np.prod(sizes)) == devs.shape[1]
        for i in range(3):
            idx = np.arange(sizes[i]).reshape([-1 if j == i else 1 for j in range(3)])
            ok = ok and bool(np.all(grid[..., i] == idx))
    except Exception:
        ok = False
    if not ok:
        return None
    return Mesh(devs.reshape((devs.shape[0],) + sizes), ("walker", "z", "x", "y"))


def solution(mesh):
    split = split_grp(mesh)
    if split is None:
        use, grp_axes, stages = mesh, "grp", ("grp",)
    else:
        use, grp_axes, stages = split, ("z", "x", "y"), (("x", "y"), "z")
    rows = ("walker",) + ((grp_axes,) if isinstance(grp_axes, str) else grp_axes)
    return jax.shard_map(
        make_on_device(stages, grp_axes),
        mesh=use,
        in_specs=(P(rows, None), P("walker"), P(), P(), P(), P(), P(), P(), P()),
        out_specs=(P("walker"), P(rows, None), P(rows, None)),
        check_vma=False,
    )
```

```python
import numpy as np
import jax
import jax.numpy as jnp
from jax import lax
from jax.experimental import pallas as pl
from jax.experimental.pallas import tpu as pltpu
from jax.sharding import Mesh
from jax.sharding import PartitionSpec as P


def orbital_kernel(col_ref, mat_ref, bias_in_ref, w_hid_t_ref, bias_hid_ref, w_out_ref, *rest):
    out_ref = rest[-1]
    rows = col_ref.shape[1]
    copies = mat_ref.shape[2] // col_ref.shape[3]
    w_hid_t = w_hid_t_ref[...]

    def one(d, r):
        col = col_ref[d, r]
        col = jnp.concatenate([col] * copies, axis=1) if copies > 1 else col
        half = (col + mat_ref[d]) + bias_in_ref[...]
        gated = (half * (1.0 + jnp.tanh(half))).astype(jnp.bfloat16)
        half = jnp.dot(w_hid_t, gated, preferred_element_type=jnp.float32) + bias_hid_ref[...]
        return jnp.sum(half * (1.0 + jnp.tanh(half)) * w_out_ref[...], axis=0, keepdims=True)

    def body(r, carry):
        out_ref[pl.ds(r, 1), :] = one(0, r) - one(1, r)
        return carry

    lax.fori_loop(0, rows, body, 0)


def orbital_rows(cols, mats, params, first, blocks, width, after=None):
    _, rows, feat, lanes = cols.shape
    count = blocks * width
    flops = 2 * rows * count * (2 * feat * feat + 12 * feat)
    operands = [cols, mats, *params]
    in_specs = [
        pl.BlockSpec((2, rows, feat, lanes), lambda j: (0, 0, 0, 0)),
        pl.BlockSpec((2, feat, width), lambda j: (0, 0, j + first)),
        pl.BlockSpec((feat, width), lambda j: (0, 0)),
        pl.BlockSpec((feat, feat), lambda j: (0, 0)),
        pl.BlockSpec((feat, width), lambda j: (0, 0)),
        pl.BlockSpec((feat, width), lambda j: (0, 0)),
    ]
    if after is not None:
        operands.append(after)
        in_specs.append(pl.BlockSpec(after.shape, lambda j: (0, 0)))
    return pl.pallas_call(
        orbital_kernel,
        grid=(blocks,),
        out_shape=jax.ShapeDtypeStruct((rows, count), jnp.float32),
        in_specs=in_specs,
        out_specs=pl.BlockSpec((rows, width), lambda j: (0, j)),
        cost_estimate=pl.CostEstimate(
            flops=flops,
            transcendentals=4 * rows * count * feat,
            bytes_accessed=4 * (2 * feat * count + rows * count),
        ),
    )(*operands)


def factor_kernel(m_in_ref, ps_ref, after_ref, pc_ref, piv_ref, scaled_ref, m_ref):
    rows, size = m_ref.shape
    lane = lax.broadcasted_iota(jnp.int32, (1, size), 1)
    lanes = lax.broadcasted_iota(jnp.int32, (rows, size), 1)
    row_idx = lax.broadcasted_iota(jnp.int32, (rows, 1), 0)
    m0 = m_in_ref[...]
    strength = ps_ref[...]
    m0 = m0 + jnp.where((row_idx % 2 == 0) & (lanes == row_idx + 1) & (row_idx < size), strength, 0.0)
    m0 = m0 - jnp.where((row_idx % 2 == 1) & (lanes == row_idx - 1) & (row_idx < size), strength, 0.0)
    m_ref[...] = m0
    below = rows - size

    def step(k, carry):
        pivots, scaled = carry
        first = 2 * k
        r0 = m_ref[pl.ds(first, 1), :]
        r1 = m_ref[pl.ds(first + 1, 1), :]
        pivot = jnp.sum(jnp.where(lane == first + 1, r0, 0.0), axis=1, keepdims=True)
        keep_lane = lane > first + 1
        even_lane = jnp.where(keep_lane, -r0 / pivot, 0.0)
        odd_lane = jnp.where(keep_lane, -r1 / pivot, 0.0)
        m = m_ref[...]
        col_even = jnp.sum(jnp.where(lanes == first, m, 0.0), axis=1, keepdims=True)
        col_odd = jnp.sum(jnp.where(lanes == first + 1, m, 0.0), axis=1, keepdims=True)
        low_even = col_even[size:]
        low_odd = col_odd[size:]
        low_lanes = lanes[size:]
        scaled = jnp.where(low_lanes == first, low_odd / pivot, scaled)
        scaled = jnp.where(low_lanes == first + 1, -low_even / pivot, scaled)
        pivots = jnp.where(lane == k, pivot, pivots)
        keep_row = row_idx > first + 1
        col_even = jnp.where(keep_row, col_even, 0.0)
        col_odd = jnp.where(keep_row, col_odd, 0.0)
        m_ref[...] = m + (col_odd * even_lane - col_even * odd_lane)
        return (pivots, scaled)

    start = (jnp.zeros((1, size), jnp.float32), jnp.zeros((below, size), jnp.float32))
    pivots, scaled = lax.fori_loop(0, size // 2, step, start)
    pc_ref[...] = m_ref[size:, :]
    piv_ref[...] = pivots
    scaled_ref[...] = scaled


def factor_augmented(matrix, strength_col, size, after):
    rows, width = matrix.shape
    below = rows - size
    vmem = pl.BlockSpec(memory_space=pltpu.VMEM)
    return pl.pallas_call(
        factor_kernel,
        out_shape=(
            jax.ShapeDtypeStruct((below, width), jnp.float32),
            jax.ShapeDtypeStruct((1, width), jnp.float32),
            jax.ShapeDtypeStruct((below, width), jnp.float32),
        ),
        in_specs=[vmem, vmem, vmem],
        out_specs=(vmem, vmem, vmem),
        scratch_shapes=[pltpu.VMEM((rows, width), jnp.float32)],
    )(matrix, strength_col, after)


def gather_rows(x, stages):
    return gather_stages(x, stages)[-1]


def gather_stages(x, stages):
    outs = []
    for axes in stages:
        x = lax.all_gather(x, axes, axis=0, tiled=True)
        outs.append(x)
    return outs


def make_on_device(stages, grp_axes):
    def on_device(feats, perm, w_left, w_right, bias_in, w_hidden, bias_hidden, w_out, pair_strength):
        groups = lax.psum(1, grp_axes)
        device = lax.axis_index(grp_axes)
        electrons = perm.shape[0]
        hid = w_left.shape[1]
        panel = 2 * pair_strength.shape[0]
        share = panel // groups
        tail = (electrons - panel) // groups
        w_both = jnp.concatenate([w_left, w_right], axis=1)
        both_own = jnp.dot(feats, w_both, preferred_element_type=jnp.float32).astype(jnp.bfloat16)
        both_every = gather_rows(both_own, stages)
        width = panel
        lanes = 128

        def columns(rows_both):
            stacked = jnp.stack([rows_both[:, :hid], rows_both[:, hid:]])[..., None]
            return jnp.broadcast_to(stacked, stacked.shape[:-1] + (lanes,))

        def transposed(rows_both):
            return jnp.stack([rows_both[:, hid:].T, rows_both[:, :hid].T])

        params = (
            jnp.broadcast_to(0.5 * bias_in[:, None], (hid, width)),
            (w_hidden.T * 0.5).astype(w_hidden.dtype),
            jnp.broadcast_to(0.5 * bias_hidden[:, None], (hid, width)),
            jnp.broadcast_to(w_out[:, None], (hid, width)),
        )
        top_both = 0.5 * jnp.take(both_every, perm[:panel], axis=0).astype(jnp.float32)
        top_own = lax.dynamic_slice_in_dim(top_both, device * share, share, 0)
        top_rows = orbital_rows(columns(top_own), transposed(top_both), params, 0, 1, width)
        pad = (-share) % 8
        top_padded = jnp.pad(top_rows, ((0, pad), (0, 0)))
        partial = gather_stages(top_padded, stages)
        gathered = partial[-1]
        late_every, _ = lax.optimization_barrier((both_every, partial[0]))
        halves = 0.5 * jnp.take(late_every, perm, axis=0).astype(jnp.float32)
        mats = transposed(halves)
        tail_own = lax.dynamic_slice_in_dim(halves, panel + device * tail, tail, 0)
        tail_cols = columns(tail_own)
        block_rows = gathered.reshape(groups, share + pad, panel)[:, :share, :].reshape(panel, panel)
        blocks = electrons // width
        early = 1
        below_own = orbital_rows(tail_cols, mats, params, 0, 1, width)
        trailing_a = orbital_rows(tail_cols, mats, params, 1, early, width)
        extra = (-tail) % 8
        augmented = jnp.concatenate(
            [block_rows, below_own, jnp.zeros((extra, panel), jnp.float32)], axis=0
        )
        strength_col = jnp.concatenate(
            [jnp.repeat(pair_strength, 2), jnp.zeros((tail + extra,), jnp.float32)]
        )[:, None]
        pc, piv_row, scaled = factor_augmented(augmented, strength_col, panel, trailing_a[:8, :128])
        pivots = piv_row[0, : panel // 2]
        log_pivot = jnp.log(jnp.abs(pivots))
        panel_own = pc[:tail]
        scaled_own = scaled[:tail]
        scaled_all = gather_rows(scaled_own, stages)
        trailing_b = orbital_rows(
            tail_cols, mats, params, 1 + early, blocks - 1 - early, width, after=piv_row
        )
        trailing_own = jnp.concatenate([trailing_a, trailing_b], axis=1)
        schur = trailing_own - jnp.dot(
            panel_own,
            scaled_all.T,
            precision=lax.Precision.HIGHEST,
        )
        return (log_pivot, panel_own, schur)

    return on_device


def split_grp(mesh):
    devs = mesh.devices
    try:
        coords = np.array([[d.coords[2], d.coords[0], d.coords[1]] for d in devs[0]])
        sizes = tuple(len(np.unique(coords[:, i])) for i in range(3))
        grid = coords.reshape(sizes + (3,))
        ok = int(np.prod(sizes)) == devs.shape[1]
        for i in range(3):
            idx = np.arange(sizes[i]).reshape([-1 if j == i else 1 for j in range(3)])
            ok = ok and bool(np.all(grid[..., i] == idx))
    except Exception:
        ok = False
    if not ok:
        return None
    return Mesh(devs.reshape((devs.shape[0],) + sizes), ("walker", "z", "x", "y"))


def solution(mesh):
    split = split_grp(mesh)
    if split is None:
        use, grp_axes, stages = mesh, "grp", ("grp",)
    else:
        use, grp_axes, stages = split, ("z", "x", "y"), (("x", "y"), "z")
    rows = ("walker",) + ((grp_axes,) if isinstance(grp_axes, str) else grp_axes)
    return jax.shard_map(
        make_on_device(stages, grp_axes),
        mesh=use,
        in_specs=(P(rows, None), P("walker"), P(), P(), P(), P(), P(), P(), P()),
        out_specs=(P("walker"), P(rows, None), P(rows, None)),
        check_vma=False,
    )
```

```python
import numpy as np
import jax
import jax.numpy as jnp
from jax import lax
from jax.experimental import pallas as pl
from jax.experimental.pallas import tpu as pltpu
from jax.sharding import Mesh
from jax.sharding import PartitionSpec as P


def orbital_kernel(col_ref, mat_ref, bias_in_ref, w_hid_t_ref, bias_hid_ref, w_out_ref, *rest):
    out_ref = rest[-1]
    rows = col_ref.shape[1]
    copies = mat_ref.shape[2] // col_ref.shape[3]
    w_hid_t = w_hid_t_ref[...]

    def one(d, r):
        col = col_ref[d, r]
        col = jnp.concatenate([col] * copies, axis=1) if copies > 1 else col
        half = (col + mat_ref[d]) + bias_in_ref[...]
        gated = (half * (1.0 + jnp.tanh(half))).astype(jnp.bfloat16)
        half = jnp.dot(w_hid_t, gated, preferred_element_type=jnp.float32) + bias_hid_ref[...]
        return jnp.sum(half * (1.0 + jnp.tanh(half)) * w_out_ref[...], axis=0, keepdims=True)

    def body(r, carry):
        out_ref[pl.ds(r, 1), :] = one(0, r) - one(1, r)
        return carry

    lax.fori_loop(0, rows, body, 0)


def orbital_rows(cols, mats, params, first, blocks, width, after=None):
    _, rows, feat, lanes = cols.shape
    count = blocks * width
    flops = 2 * rows * count * (2 * feat * feat + 12 * feat)
    operands = [cols, mats, *params]
    in_specs = [
        pl.BlockSpec((2, rows, feat, lanes), lambda j: (0, 0, 0, 0)),
        pl.BlockSpec((2, feat, width), lambda j: (0, 0, j + first)),
        pl.BlockSpec((feat, width), lambda j: (0, 0)),
        pl.BlockSpec((feat, feat), lambda j: (0, 0)),
        pl.BlockSpec((feat, width), lambda j: (0, 0)),
        pl.BlockSpec((feat, width), lambda j: (0, 0)),
    ]
    if after is not None:
        operands.append(after)
        in_specs.append(pl.BlockSpec(after.shape, lambda j: (0, 0)))
    return pl.pallas_call(
        orbital_kernel,
        grid=(blocks,),
        out_shape=jax.ShapeDtypeStruct((rows, count), jnp.float32),
        in_specs=in_specs,
        out_specs=pl.BlockSpec((rows, width), lambda j: (0, j)),
        cost_estimate=pl.CostEstimate(
            flops=flops,
            transcendentals=4 * rows * count * feat,
            bytes_accessed=4 * (2 * feat * count + rows * count),
        ),
    )(*operands)


def factor_kernel(m_in_ref, ps_ref, after_ref, pc_ref, piv_ref, scaled_ref, m_ref):
    rows, size = m_ref.shape
    half = size // 2
    below = rows - size
    lanes_all = lax.broadcasted_iota(jnp.int32, (rows, size), 1)
    row_all = lax.broadcasted_iota(jnp.int32, (rows, 1), 0)
    m0 = m_in_ref[...]
    strength = ps_ref[...]
    m0 = m0 + jnp.where((row_all % 2 == 0) & (lanes_all == row_all + 1) & (row_all < size), strength, 0.0)
    m0 = m0 - jnp.where((row_all % 2 == 1) & (lanes_all == row_all - 1) & (row_all < size), strength, 0.0)
    m_ref[...] = m0
    lane_full = lax.broadcasted_iota(jnp.int32, (1, size), 1)
    low_lanes = lax.broadcasted_iota(jnp.int32, (below, size), 1)

    def make_step(lo):
        sub_rows, sub_cols = rows - lo, size - lo
        reach = min(half, sub_cols)
        lane = lax.broadcasted_iota(jnp.int32, (1, sub_cols), 1) + lo
        lanes = lax.broadcasted_iota(jnp.int32, (sub_rows, reach), 1) + lo
        row_idx = lax.broadcasted_iota(jnp.int32, (sub_rows, 1), 0) + lo

        def step(k, carry):
            pivots, scaled = carry
            first = 2 * k
            r0 = m_ref[pl.ds(first, 1), :][:, lo:]
            r1 = m_ref[pl.ds(first + 1, 1), :][:, lo:]
            pivot = jnp.sum(jnp.where(lane == first + 1, r0, 0.0), axis=1, keepdims=True)
            keep_lane = lane > first + 1
            even_lane = jnp.where(keep_lane, -r0 / pivot, 0.0)
            odd_lane = jnp.where(keep_lane, -r1 / pivot, 0.0)
            m = m_ref[lo:, lo:]
            window = m[:, :reach]
            col_even = jnp.sum(jnp.where(lanes == first, window, 0.0), axis=1, keepdims=True)
            col_odd = jnp.sum(jnp.where(lanes == first + 1, window, 0.0), axis=1, keepdims=True)
            low_even = col_even[size - lo:]
            low_odd = col_odd[size - lo:]
            scaled = jnp.where(low_lanes == first, low_odd / pivot, scaled)
            scaled = jnp.where(low_lanes == first + 1, -low_even / pivot, scaled)
            pivots = jnp.where(lane_full == k, pivot, pivots)
            keep_row = row_idx > first + 1
            col_even = jnp.where(keep_row, col_even, 0.0)
            col_odd = jnp.where(keep_row, col_odd, 0.0)
            m_ref[lo:, lo:] = m + (col_odd * even_lane - col_even * odd_lane)
            return (pivots, scaled)

        return step

    carry = (jnp.zeros((1, size), jnp.float32), jnp.zeros((below, size), jnp.float32))
    carry = lax.fori_loop(0, half // 2, make_step(0), carry)
    pivots, scaled = lax.fori_loop(half // 2, size // 2, make_step(half), carry)
    pc_ref[...] = m_ref[size:, :]
    piv_ref[...] = pivots
    scaled_ref[...] = scaled


def factor_augmented(matrix, strength_col, size, after):
    rows, width = matrix.shape
    below = rows - size
    vmem = pl.BlockSpec(memory_space=pltpu.VMEM)
    return pl.pallas_call(
        factor_kernel,
        out_shape=(
            jax.ShapeDtypeStruct((below, width), jnp.float32),
            jax.ShapeDtypeStruct((1, width), jnp.float32),
            jax.ShapeDtypeStruct((below, width), jnp.float32),
        ),
        in_specs=[vmem, vmem, vmem],
        out_specs=(vmem, vmem, vmem),
        scratch_shapes=[pltpu.VMEM((rows, width), jnp.float32)],
    )(matrix, strength_col, after)


def gather_rows(x, stages):
    return gather_stages(x, stages)[-1]


def gather_stages(x, stages):
    outs = []
    for axes in stages:
        x = lax.all_gather(x, axes, axis=0, tiled=True)
        outs.append(x)
    return outs


def make_on_device(stages, grp_axes):
    def on_device(feats, perm, w_left, w_right, bias_in, w_hidden, bias_hidden, w_out, pair_strength):
        groups = lax.psum(1, grp_axes)
        device = lax.axis_index(grp_axes)
        electrons = perm.shape[0]
        hid = w_left.shape[1]
        panel = 2 * pair_strength.shape[0]
        share = panel // groups
        tail = (electrons - panel) // groups
        w_both = jnp.concatenate([w_left, w_right], axis=1)
        both_own = jnp.dot(feats, w_both, preferred_element_type=jnp.float32).astype(jnp.bfloat16)
        both_every = gather_rows(both_own, stages)
        width = panel
        lanes = 128

        def columns(rows_both):
            stacked = jnp.stack([rows_both[:, :hid], rows_both[:, hid:]])[..., None]
            return jnp.broadcast_to(stacked, stacked.shape[:-1] + (lanes,))

        def transposed(rows_both):
            return jnp.stack([rows_both[:, hid:].T, rows_both[:, :hid].T])

        params = (
            jnp.broadcast_to(0.5 * bias_in[:, None], (hid, width)),
            (w_hidden.T * 0.5).astype(w_hidden.dtype),
            jnp.broadcast_to(0.5 * bias_hidden[:, None], (hid, width)),
            jnp.broadcast_to(w_out[:, None], (hid, width)),
        )
        top_both = 0.5 * jnp.take(both_every, perm[:panel], axis=0).astype(jnp.float32)
        top_own = lax.dynamic_slice_in_dim(top_both, device * share, share, 0)
        top_rows = orbital_rows(columns(top_own), transposed(top_both), params, 0, 1, width)
        pad = (-share) % 8
        top_padded = jnp.pad(top_rows, ((0, pad), (0, 0)))
        partial = gather_stages(top_padded, stages)
        gathered = partial[-1]
        late_every, _ = lax.optimization_barrier((both_every, partial[0]))
        halves = 0.5 * jnp.take(late_every, perm, axis=0).astype(jnp.float32)
        mats = transposed(halves)
        tail_own = lax.dynamic_slice_in_dim(halves, panel + device * tail, tail, 0)
        tail_cols = columns(tail_own)
        block_rows = gathered.reshape(groups, share + pad, panel)[:, :share, :].reshape(panel, panel)
        blocks = electrons // width
        early = 1
        below_own = orbital_rows(tail_cols, mats, params, 0, 1, width)
        trailing_a = orbital_rows(tail_cols, mats, params, 1, early, width)
        extra = (-tail) % 8
        augmented = jnp.concatenate(
            [block_rows, below_own, jnp.zeros((extra, panel), jnp.float32)], axis=0
        )
        strength_col = jnp.concatenate(
            [jnp.repeat(pair_strength, 2), jnp.zeros((tail + extra,), jnp.float32)]
        )[:, None]
        pc, piv_row, scaled = factor_augmented(augmented, strength_col, panel, trailing_a[:8, :128])
        pivots = piv_row[0, : panel // 2]
        log_pivot = jnp.log(jnp.abs(pivots))
        panel_own = pc[:tail]
        scaled_own = scaled[:tail]
        scaled_all = gather_rows(scaled_own, stages)
        trailing_b = orbital_rows(
            tail_cols, mats, params, 1 + early, blocks - 1 - early, width, after=piv_row
        )
        trailing_own = jnp.concatenate([trailing_a, trailing_b], axis=1)
        schur = trailing_own - jnp.dot(
            panel_own,
            scaled_all.T,
            precision=lax.Precision.HIGHEST,
        )
        return (log_pivot, panel_own, schur)

    return on_device


def split_grp(mesh):
    devs = mesh.devices
    try:
        coords = np.array([[d.coords[2], d.coords[0], d.coords[1]] for d in devs[0]])
        sizes = tuple(len(np.unique(coords[:, i])) for i in range(3))
        grid = coords.reshape(sizes + (3,))
        ok = int(np.prod(sizes)) == devs.shape[1]
        for i in range(3):
            idx = np.arange(sizes[i]).reshape([-1 if j == i else 1 for j in range(3)])
            ok = ok and bool(np.all(grid[..., i] == idx))
    except Exception:
        ok = False
    if not ok:
        return None
    return Mesh(devs.reshape((devs.shape[0],) + sizes), ("walker", "z", "x", "y"))


def solution(mesh):
    split = split_grp(mesh)
    if split is None:
        use, grp_axes, stages = mesh, "grp", ("grp",)
    else:
        use, grp_axes, stages = split, ("z", "x", "y"), (("x", "y"), "z")
    rows = ("walker",) + ((grp_axes,) if isinstance(grp_axes, str) else grp_axes)
    return jax.shard_map(
        make_on_device(stages, grp_axes),
        mesh=use,
        in_specs=(P(rows, None), P("walker"), P(), P(), P(), P(), P(), P(), P()),
        out_specs=(P("walker"), P(rows, None), P(rows, None)),
        check_vma=False,
    )
```

```python
import numpy as np
import jax
import jax.numpy as jnp
from jax import lax
from jax.experimental import pallas as pl
from jax.experimental.pallas import tpu as pltpu
from jax.sharding import Mesh
from jax.sharding import PartitionSpec as P


def orbital_kernel(col_ref, mat_ref, bias_in_ref, w_hid_t_ref, bias_hid_ref, w_out_ref, *rest):
    out_ref = rest[-1]
    rows = col_ref.shape[1]
    copies = mat_ref.shape[2] // col_ref.shape[3]
    w_hid_t = w_hid_t_ref[...]

    def one(d, r):
        col = col_ref[d, r]
        col = jnp.concatenate([col] * copies, axis=1) if copies > 1 else col
        half = (col + mat_ref[d]) + bias_in_ref[...]
        gated = (half * (1.0 + jnp.tanh(half))).astype(jnp.bfloat16)
        half = jnp.dot(w_hid_t, gated, preferred_element_type=jnp.float32) + bias_hid_ref[...]
        return jnp.sum(half * (1.0 + jnp.tanh(half)) * w_out_ref[...], axis=0, keepdims=True)

    def body(r, carry):
        out_ref[pl.ds(r, 1), :] = one(0, r) - one(1, r)
        return carry

    lax.fori_loop(0, rows, body, 0)


def orbital_rows(cols, mats, params, first, blocks, width, after=None):
    _, rows, feat, lanes = cols.shape
    count = blocks * width
    flops = 2 * rows * count * (2 * feat * feat + 12 * feat)
    operands = [cols, mats, *params]
    in_specs = [
        pl.BlockSpec((2, rows, feat, lanes), lambda j: (0, 0, 0, 0)),
        pl.BlockSpec((2, feat, width), lambda j: (0, 0, j + first)),
        pl.BlockSpec((feat, width), lambda j: (0, 0)),
        pl.BlockSpec((feat, feat), lambda j: (0, 0)),
        pl.BlockSpec((feat, width), lambda j: (0, 0)),
        pl.BlockSpec((feat, width), lambda j: (0, 0)),
    ]
    if after is not None:
        operands.append(after)
        in_specs.append(pl.BlockSpec(after.shape, lambda j: (0, 0)))
    return pl.pallas_call(
        orbital_kernel,
        grid=(blocks,),
        out_shape=jax.ShapeDtypeStruct((rows, count), jnp.float32),
        in_specs=in_specs,
        out_specs=pl.BlockSpec((rows, width), lambda j: (0, j)),
        cost_estimate=pl.CostEstimate(
            flops=flops,
            transcendentals=4 * rows * count * feat,
            bytes_accessed=4 * (2 * feat * count + rows * count),
        ),
    )(*operands)


def factor_kernel(m_in_ref, ps_ref, after_ref, pc_ref, piv_ref, scaled_ref, m_ref):
    rows, size = m_ref.shape
    half = size // 2
    below = rows - size
    lanes_all = lax.broadcasted_iota(jnp.int32, (rows, size), 1)
    row_all = lax.broadcasted_iota(jnp.int32, (rows, 1), 0)
    m0 = m_in_ref[...]
    strength = ps_ref[...]
    m0 = m0 + jnp.where((row_all % 2 == 0) & (lanes_all == row_all + 1) & (row_all < size), strength, 0.0)
    m0 = m0 - jnp.where((row_all % 2 == 1) & (lanes_all == row_all - 1) & (row_all < size), strength, 0.0)
    m_ref[...] = m0
    lane_full = lax.broadcasted_iota(jnp.int32, (1, size), 1)
    low_lanes = lax.broadcasted_iota(jnp.int32, (below, size), 1)

    def make_step(lo):
        sub_rows, sub_cols = rows - lo, size - lo
        reach = min(half, sub_cols)
        lane = lax.broadcasted_iota(jnp.int32, (1, sub_cols), 1) + lo
        lanes = lax.broadcasted_iota(jnp.int32, (sub_rows, reach), 1) + lo
        row_idx = lax.broadcasted_iota(jnp.int32, (sub_rows, 1), 0) + lo

        def step(k, carry):
            pivots, scaled = carry
            first = 2 * k
            r0 = m_ref[pl.ds(first, 1), :][:, lo:]
            r1 = m_ref[pl.ds(first + 1, 1), :][:, lo:]
            pivot = jnp.sum(jnp.where(lane == first + 1, r0, 0.0), axis=1, keepdims=True)
            keep_lane = lane > first + 1
            even_lane = jnp.where(keep_lane, -r0 / pivot, 0.0)
            odd_lane = jnp.where(keep_lane, -r1 / pivot, 0.0)
            m = m_ref[lo:, lo:]
            window = m[:, :reach]
            col_even = jnp.sum(jnp.where(lanes == first, window, 0.0), axis=1, keepdims=True)
            col_odd = jnp.sum(jnp.where(lanes == first + 1, window, 0.0), axis=1, keepdims=True)
            low_even = col_even[size - lo:]
            low_odd = col_odd[size - lo:]
            scaled = jnp.where(low_lanes == first, low_odd / pivot, scaled)
            scaled = jnp.where(low_lanes == first + 1, -low_even / pivot, scaled)
            pivots = jnp.where(lane_full == k, pivot, pivots)
            keep_row = row_idx > first + 1
            col_even = jnp.where(keep_row, col_even, 0.0)
            col_odd = jnp.where(keep_row, col_odd, 0.0)
            m_ref[lo:, lo:] = m + (col_odd * even_lane - col_even * odd_lane)
            return (pivots, scaled)

        return step

    carry = (jnp.zeros((1, size), jnp.float32), jnp.zeros((below, size), jnp.float32))
    carry = lax.fori_loop(0, half // 2, make_step(0), carry, unroll=2)
    pivots, scaled = lax.fori_loop(half // 2, size // 2, make_step(half), carry, unroll=2)
    pc_ref[...] = m_ref[size:, :]
    piv_ref[...] = pivots
    scaled_ref[...] = scaled


def factor_augmented(matrix, strength_col, size, after):
    rows, width = matrix.shape
    below = rows - size
    vmem = pl.BlockSpec(memory_space=pltpu.VMEM)
    return pl.pallas_call(
        factor_kernel,
        out_shape=(
            jax.ShapeDtypeStruct((below, width), jnp.float32),
            jax.ShapeDtypeStruct((1, width), jnp.float32),
            jax.ShapeDtypeStruct((below, width), jnp.float32),
        ),
        in_specs=[vmem, vmem, vmem],
        out_specs=(vmem, vmem, vmem),
        scratch_shapes=[pltpu.VMEM((rows, width), jnp.float32)],
    )(matrix, strength_col, after)


def gather_rows(x, stages):
    return gather_stages(x, stages)[-1]


def gather_stages(x, stages):
    outs = []
    for axes in stages:
        x = lax.all_gather(x, axes, axis=0, tiled=True)
        outs.append(x)
    return outs


def make_on_device(stages, grp_axes):
    def on_device(feats, perm, w_left, w_right, bias_in, w_hidden, bias_hidden, w_out, pair_strength):
        groups = lax.psum(1, grp_axes)
        device = lax.axis_index(grp_axes)
        electrons = perm.shape[0]
        hid = w_left.shape[1]
        panel = 2 * pair_strength.shape[0]
        share = panel // groups
        tail = (electrons - panel) // groups
        w_both = jnp.concatenate([w_left, w_right], axis=1)
        both_own = jnp.dot(feats, w_both, preferred_element_type=jnp.float32).astype(jnp.bfloat16)
        both_every = gather_rows(both_own, stages)
        width = panel
        lanes = 128

        def columns(rows_both):
            stacked = jnp.stack([rows_both[:, :hid], rows_both[:, hid:]])[..., None]
            return jnp.broadcast_to(stacked, stacked.shape[:-1] + (lanes,))

        def transposed(rows_both):
            return jnp.stack([rows_both[:, hid:].T, rows_both[:, :hid].T])

        params = (
            jnp.broadcast_to(0.5 * bias_in[:, None], (hid, width)),
            (w_hidden.T * 0.5).astype(w_hidden.dtype),
            jnp.broadcast_to(0.5 * bias_hidden[:, None], (hid, width)),
            jnp.broadcast_to(w_out[:, None], (hid, width)),
        )
        top_both = 0.5 * jnp.take(both_every, perm[:panel], axis=0).astype(jnp.float32)
        top_own = lax.dynamic_slice_in_dim(top_both, device * share, share, 0)
        top_rows = orbital_rows(columns(top_own), transposed(top_both), params, 0, 1, width)
        pad = (-share) % 8
        top_padded = jnp.pad(top_rows, ((0, pad), (0, 0)))
        partial = gather_stages(top_padded, stages)
        gathered = partial[-1]
        late_every, _ = lax.optimization_barrier((both_every, partial[0]))
        halves = 0.5 * jnp.take(late_every, perm, axis=0).astype(jnp.float32)
        mats = transposed(halves)
        tail_own = lax.dynamic_slice_in_dim(halves, panel + device * tail, tail, 0)
        tail_cols = columns(tail_own)
        block_rows = gathered.reshape(groups, share + pad, panel)[:, :share, :].reshape(panel, panel)
        blocks = electrons // width
        early = 1
        first_part = orbital_rows(tail_cols, mats, params, 0, 1 + early, width)
        below_own = first_part[:, :panel]
        trailing_a = first_part[:, panel:]
        extra = (-tail) % 8
        augmented = jnp.concatenate(
            [block_rows, below_own, jnp.zeros((extra, panel), jnp.float32)], axis=0
        )
        strength_col = jnp.concatenate(
            [jnp.repeat(pair_strength, 2), jnp.zeros((tail + extra,), jnp.float32)]
        )[:, None]
        pc, piv_row, scaled = factor_augmented(augmented, strength_col, panel, trailing_a[:8, :128])
        pivots = piv_row[0, : panel // 2]
        log_pivot = jnp.log(jnp.abs(pivots))
        panel_own = pc[:tail]
        scaled_own = scaled[:tail]
        scaled_all = gather_rows(scaled_own, stages)
        trailing_b = orbital_rows(
            tail_cols, mats, params, 1 + early, blocks - 1 - early, width, after=piv_row
        )
        trailing_own = jnp.concatenate([trailing_a, trailing_b], axis=1)
        schur = trailing_own - jnp.dot(
            panel_own,
            scaled_all.T,
            precision=lax.Precision.HIGHEST,
        )
        return (log_pivot, panel_own, schur)

    return on_device


def split_grp(mesh):
    devs = mesh.devices
    try:
        coords = np.array([[d.coords[2], d.coords[0], d.coords[1]] for d in devs[0]])
        sizes = tuple(len(np.unique(coords[:, i])) for i in range(3))
        grid = coords.reshape(sizes + (3,))
        ok = int(np.prod(sizes)) == devs.shape[1]
        for i in range(3):
            idx = np.arange(sizes[i]).reshape([-1 if j == i else 1 for j in range(3)])
            ok = ok and bool(np.all(grid[..., i] == idx))
    except Exception:
        ok = False
    if not ok:
        return None
    return Mesh(devs.reshape((devs.shape[0],) + sizes), ("walker", "z", "x", "y"))


def solution(mesh):
    split = split_grp(mesh)
    if split is None:
        use, grp_axes, stages = mesh, "grp", ("grp",)
    else:
        use, grp_axes, stages = split, ("z", "x", "y"), (("x", "y"), "z")
    rows = ("walker",) + ((grp_axes,) if isinstance(grp_axes, str) else grp_axes)
    return jax.shard_map(
        make_on_device(stages, grp_axes),
        mesh=use,
        in_specs=(P(rows, None), P("walker"), P(), P(), P(), P(), P(), P(), P()),
        out_specs=(P("walker"), P(rows, None), P(rows, None)),
        check_vma=False,
    )
```

```python
import numpy as np
import jax
import jax.numpy as jnp
from jax import lax
from jax.experimental import pallas as pl
from jax.experimental.pallas import tpu as pltpu
from jax.sharding import Mesh
from jax.sharding import PartitionSpec as P


def orbital_kernel(col_ref, mat_ref, bias_in_ref, w_hid_t_ref, bias_hid_ref, w_out_ref, *rest):
    out_ref = rest[-1]
    rows = col_ref.shape[1]
    copies = mat_ref.shape[2] // col_ref.shape[3]
    w_hid_t = w_hid_t_ref[...]

    def one(d, r):
        col = col_ref[d, r]
        col = jnp.concatenate([col] * copies, axis=1) if copies > 1 else col
        half = (col + mat_ref[d]) + bias_in_ref[...]
        gated = (half * (1.0 + jnp.tanh(half))).astype(jnp.bfloat16)
        half = jnp.dot(w_hid_t, gated, preferred_element_type=jnp.float32) + bias_hid_ref[...]
        return jnp.sum(half * (1.0 + jnp.tanh(half)) * w_out_ref[...], axis=0, keepdims=True)

    def body(r, carry):
        out_ref[pl.ds(r, 1), :] = one(0, r) - one(1, r)
        return carry

    lax.fori_loop(0, rows, body, 0)


def orbital_rows(cols, mats, params, first, blocks, width, after=None):
    _, rows, feat, lanes = cols.shape
    count = blocks * width
    flops = 2 * rows * count * (2 * feat * feat + 12 * feat)
    operands = [cols, mats, *params]
    in_specs = [
        pl.BlockSpec((2, rows, feat, lanes), lambda j: (0, 0, 0, 0)),
        pl.BlockSpec((2, feat, width), lambda j: (0, 0, j + first)),
        pl.BlockSpec((feat, width), lambda j: (0, 0)),
        pl.BlockSpec((feat, feat), lambda j: (0, 0)),
        pl.BlockSpec((feat, width), lambda j: (0, 0)),
        pl.BlockSpec((feat, width), lambda j: (0, 0)),
    ]
    if after is not None:
        operands.append(after)
        in_specs.append(pl.BlockSpec(after.shape, lambda j: (0, 0)))
    return pl.pallas_call(
        orbital_kernel,
        grid=(blocks,),
        out_shape=jax.ShapeDtypeStruct((rows, count), jnp.float32),
        in_specs=in_specs,
        out_specs=pl.BlockSpec((rows, width), lambda j: (0, j)),
        cost_estimate=pl.CostEstimate(
            flops=flops,
            transcendentals=4 * rows * count * feat,
            bytes_accessed=4 * (2 * feat * count + rows * count),
        ),
    )(*operands)


def factor_kernel(block_ref, first_ref, ps_ref, pc_ref, piv_ref, scaled_ref, m_ref):
    rows, size = m_ref.shape
    half = size // 2
    below = rows - size
    own = first_ref.shape[0]
    lanes_blk = lax.broadcasted_iota(jnp.int32, (size, size), 1)
    row_blk = lax.broadcasted_iota(jnp.int32, (size, 1), 0)
    strength = ps_ref[...]
    m0 = block_ref[...]
    m0 = m0 + jnp.where((row_blk % 2 == 0) & (lanes_blk == row_blk + 1), strength, 0.0)
    m0 = m0 - jnp.where((row_blk % 2 == 1) & (lanes_blk == row_blk - 1), strength, 0.0)
    m_ref[:size, :] = m0
    m_ref[size:, :] = jnp.zeros((below, size), jnp.float32)
    m_ref[size:size + own, :] = first_ref[:, :size]
    lane_full = lax.broadcasted_iota(jnp.int32, (1, size), 1)
    low_lanes = lax.broadcasted_iota(jnp.int32, (below, size), 1)

    def make_step(lo):
        sub_rows, sub_cols = rows - lo, size - lo
        reach = min(half, sub_cols)
        lane = lax.broadcasted_iota(jnp.int32, (1, sub_cols), 1) + lo
        lanes = lax.broadcasted_iota(jnp.int32, (sub_rows, reach), 1) + lo
        row_idx = lax.broadcasted_iota(jnp.int32, (sub_rows, 1), 0) + lo

        def step(k, carry):
            pivots, scaled = carry
            first = 2 * k
            r0 = m_ref[pl.ds(first, 1), :][:, lo:]
            r1 = m_ref[pl.ds(first + 1, 1), :][:, lo:]
            pivot = jnp.sum(jnp.where(lane == first + 1, r0, 0.0), axis=1, keepdims=True)
            keep_lane = lane > first + 1
            even_lane = jnp.where(keep_lane, -r0 / pivot, 0.0)
            odd_lane = jnp.where(keep_lane, -r1 / pivot, 0.0)
            m = m_ref[lo:, lo:]
            window = m[:, :reach]
            col_even = jnp.sum(jnp.where(lanes == first, window, 0.0), axis=1, keepdims=True)
            col_odd = jnp.sum(jnp.where(lanes == first + 1, window, 0.0), axis=1, keepdims=True)
            low_even = col_even[size - lo:]
            low_odd = col_odd[size - lo:]
            scaled = jnp.where(low_lanes == first, low_odd / pivot, scaled)
            scaled = jnp.where(low_lanes == first + 1, -low_even / pivot, scaled)
            pivots = jnp.where(lane_full == k, pivot, pivots)
            keep_row = row_idx > first + 1
            col_even = jnp.where(keep_row, col_even, 0.0)
            col_odd = jnp.where(keep_row, col_odd, 0.0)
            m_ref[lo:, lo:] = m + (col_odd * even_lane - col_even * odd_lane)
            return (pivots, scaled)

        return step

    carry = (jnp.zeros((1, size), jnp.float32), jnp.zeros((below, size), jnp.float32))
    carry = lax.fori_loop(0, half // 2, make_step(0), carry, unroll=2)
    pivots, scaled = lax.fori_loop(half // 2, size // 2, make_step(half), carry, unroll=2)
    pc_ref[...] = m_ref[size:, :]
    piv_ref[...] = pivots
    scaled_ref[...] = scaled


def factor_augmented(block, first, strength_col, below):
    size, width = block.shape
    rows = size + below
    vmem = pl.BlockSpec(memory_space=pltpu.VMEM)
    return pl.pallas_call(
        factor_kernel,
        out_shape=(
            jax.ShapeDtypeStruct((below, width), jnp.float32),
            jax.ShapeDtypeStruct((1, width), jnp.float32),
            jax.ShapeDtypeStruct((below, width), jnp.float32),
        ),
        in_specs=[vmem, vmem, vmem],
        out_specs=(vmem, vmem, vmem),
        scratch_shapes=[pltpu.VMEM((rows, width), jnp.float32)],
    )(block, first, strength_col)


def gather_rows(x, stages):
    return gather_stages(x, stages)[-1]


def gather_stages(x, stages):
    outs = []
    for axes in stages:
        x = lax.all_gather(x, axes, axis=0, tiled=True)
        outs.append(x)
    return outs


def make_on_device(stages, grp_axes):
    def on_device(feats, perm, w_left, w_right, bias_in, w_hidden, bias_hidden, w_out, pair_strength):
        groups = lax.psum(1, grp_axes)
        device = lax.axis_index(grp_axes)
        electrons = perm.shape[0]
        hid = w_left.shape[1]
        panel = 2 * pair_strength.shape[0]
        share = panel // groups
        tail = (electrons - panel) // groups
        w_both = jnp.concatenate([w_left, w_right], axis=1)
        both_own = jnp.dot(feats, w_both, preferred_element_type=jnp.float32).astype(jnp.bfloat16)
        both_every = gather_rows(both_own, stages)
        width = panel
        lanes = 128

        def columns(rows_both):
            stacked = jnp.stack([rows_both[:, :hid], rows_both[:, hid:]])[..., None]
            return jnp.broadcast_to(stacked, stacked.shape[:-1] + (lanes,))

        def transposed(rows_both):
            return jnp.stack([rows_both[:, hid:].T, rows_both[:, :hid].T])

        params = (
            jnp.broadcast_to(0.5 * bias_in[:, None], (hid, width)),
            (w_hidden.T * 0.5).astype(w_hidden.dtype),
            jnp.broadcast_to(0.5 * bias_hidden[:, None], (hid, width)),
            jnp.broadcast_to(w_out[:, None], (hid, width)),
        )
        top_both = 0.5 * jnp.take(both_every, perm[:panel], axis=0).astype(jnp.float32)
        top_own = lax.dynamic_slice_in_dim(top_both, device * share, share, 0)
        top_rows = orbital_rows(columns(top_own), transposed(top_both), params, 0, 1, width)
        pad = (-share) % 8
        top_padded = jnp.pad(top_rows, ((0, pad), (0, 0)))
        partial = gather_stages(top_padded, stages)
        gathered = partial[-1]
        late_every, _ = lax.optimization_barrier((both_every, partial[0]))
        halves = 0.5 * jnp.take(late_every, perm, axis=0).astype(jnp.float32)
        mats = transposed(halves)
        tail_own = lax.dynamic_slice_in_dim(halves, panel + device * tail, tail, 0)
        tail_cols = columns(tail_own)
        block_rows = gathered.reshape(groups, share + pad, panel)[:, :share, :].reshape(panel, panel)
        blocks = electrons // width
        early = 1
        first_part = orbital_rows(tail_cols, mats, params, 0, 1 + early, width)
        trailing_a = first_part[:, panel:]
        extra = (-tail) % 8
        strength_col = jnp.repeat(pair_strength, 2)[:, None]
        pc, piv_row, scaled = factor_augmented(block_rows, first_part, strength_col, tail + extra)
        pivots = piv_row[0, : panel // 2]
        log_pivot = jnp.log(jnp.abs(pivots))
        panel_own = pc[:tail]
        scaled_own = scaled[:tail]
        scaled_all = gather_rows(scaled_own, stages)
        trailing_b = orbital_rows(
            tail_cols, mats, params, 1 + early, blocks - 1 - early, width, after=piv_row
        )
        trailing_own = jnp.concatenate([trailing_a, trailing_b], axis=1)
        schur = trailing_own - jnp.dot(
            panel_own,
            scaled_all.T,
            precision=lax.Precision.HIGHEST,
        )
        return (log_pivot, panel_own, schur)

    return on_device


def split_grp(mesh):
    devs = mesh.devices
    try:
        coords = np.array([[d.coords[2], d.coords[0], d.coords[1]] for d in devs[0]])
        sizes = tuple(len(np.unique(coords[:, i])) for i in range(3))
        grid = coords.reshape(sizes + (3,))
        ok = int(np.prod(sizes)) == devs.shape[1]
        for i in range(3):
            idx = np.arange(sizes[i]).reshape([-1 if j == i else 1 for j in range(3)])
            ok = ok and bool(np.all(grid[..., i] == idx))
    except Exception:
        ok = False
    if not ok:
        return None
    return Mesh(devs.reshape((devs.shape[0],) + sizes), ("walker", "z", "x", "y"))


def solution(mesh):
    split = split_grp(mesh)
    if split is None:
        use, grp_axes, stages = mesh, "grp", ("grp",)
    else:
        use, grp_axes, stages = split, ("z", "x", "y"), (("x", "y"), "z")
    rows = ("walker",) + ((grp_axes,) if isinstance(grp_axes, str) else grp_axes)
    return jax.shard_map(
        make_on_device(stages, grp_axes),
        mesh=use,
        in_specs=(P(rows, None), P("walker"), P(), P(), P(), P(), P(), P(), P()),
        out_specs=(P("walker"), P(rows, None), P(rows, None)),
        check_vma=False,
    )
```

```python
import functools

import numpy as np
import jax
import jax.numpy as jnp
from jax import lax
from jax.experimental import pallas as pl
from jax.experimental.pallas import tpu as pltpu
from jax.sharding import Mesh
from jax.sharding import PartitionSpec as P


def orbital_kernel(col_ref, mat_ref, bias_in_ref, w_hid_t_ref, bias_hid_ref, w_out_ref, *rest):
    out_ref = rest[-1]
    rows = col_ref.shape[1]
    copies = mat_ref.shape[2] // col_ref.shape[3]
    w_hid_t = w_hid_t_ref[...]

    def one(d, r):
        col = col_ref[d, r]
        col = jnp.concatenate([col] * copies, axis=1) if copies > 1 else col
        half = (col + mat_ref[d]) + bias_in_ref[...]
        gated = (half * (1.0 + jnp.tanh(half))).astype(jnp.bfloat16)
        half = jnp.dot(w_hid_t, gated, preferred_element_type=jnp.float32) + bias_hid_ref[...]
        return jnp.sum(half * (1.0 + jnp.tanh(half)) * w_out_ref[...], axis=0, keepdims=True)

    def body(r, carry):
        out_ref[pl.ds(r, 1), :] = one(0, r) - one(1, r)
        return carry

    lax.fori_loop(0, rows, body, 0)


def orbital_rows(cols, mats, params, first, blocks, width, after=None):
    _, rows, feat, lanes = cols.shape
    count = blocks * width
    flops = 2 * rows * count * (2 * feat * feat + 12 * feat)
    operands = [cols, mats, *params]
    in_specs = [
        pl.BlockSpec((2, rows, feat, lanes), lambda j: (0, 0, 0, 0)),
        pl.BlockSpec((2, feat, width), lambda j: (0, 0, j + first)),
        pl.BlockSpec((feat, width), lambda j: (0, 0)),
        pl.BlockSpec((feat, feat), lambda j: (0, 0)),
        pl.BlockSpec((feat, width), lambda j: (0, 0)),
        pl.BlockSpec((feat, width), lambda j: (0, 0)),
    ]
    if after is not None:
        operands.append(after)
        in_specs.append(pl.BlockSpec(after.shape, lambda j: (0, 0)))
    return pl.pallas_call(
        orbital_kernel,
        grid=(blocks,),
        out_shape=jax.ShapeDtypeStruct((rows, count), jnp.float32),
        in_specs=in_specs,
        out_specs=pl.BlockSpec((rows, width), lambda j: (0, j)),
        cost_estimate=pl.CostEstimate(
            flops=flops,
            transcendentals=4 * rows * count * feat,
            bytes_accessed=4 * (2 * feat * count + rows * count),
        ),
    )(*operands)


def factor_kernel(share, block_ref, first_ref, ps_ref, pc_ref, piv_ref, scaled_ref, m_ref):
    rows, size = m_ref.shape
    half = size // 2
    below = rows - size
    own = first_ref.shape[0]
    lanes_blk = lax.broadcasted_iota(jnp.int32, (size, size), 1)
    row_blk = lax.broadcasted_iota(jnp.int32, (size, 1), 0)
    strength = ps_ref[...]
    stride = block_ref.shape[0] * share // size

    for g in range(size // share):
        m_ref[g * share:(g + 1) * share, :] = block_ref[g * stride:g * stride + share, :]
    m0 = m_ref[:size, :]
    m0 = m0 + jnp.where((row_blk % 2 == 0) & (lanes_blk == row_blk + 1), strength, 0.0)
    m0 = m0 - jnp.where((row_blk % 2 == 1) & (lanes_blk == row_blk - 1), strength, 0.0)
    m_ref[:size, :] = m0
    m_ref[size:, :] = jnp.zeros((below, size), jnp.float32)
    m_ref[size:size + own, :] = first_ref[:, :size]
    lane_full = lax.broadcasted_iota(jnp.int32, (1, size), 1)
    low_lanes = lax.broadcasted_iota(jnp.int32, (below, size), 1)

    def make_step(lo):
        sub_rows, sub_cols = rows - lo, size - lo
        reach = min(half, sub_cols)
        lane = lax.broadcasted_iota(jnp.int32, (1, sub_cols), 1) + lo
        lanes = lax.broadcasted_iota(jnp.int32, (sub_rows, reach), 1) + lo
        row_idx = lax.broadcasted_iota(jnp.int32, (sub_rows, 1), 0) + lo

        def step(k, carry):
            pivots, scaled = carry
            first = 2 * k
            r0 = m_ref[pl.ds(first, 1), :][:, lo:]
            r1 = m_ref[pl.ds(first + 1, 1), :][:, lo:]
            pivot = jnp.sum(jnp.where(lane == first + 1, r0, 0.0), axis=1, keepdims=True)
            keep_lane = lane > first + 1
            even_lane = jnp.where(keep_lane, -r0 / pivot, 0.0)
            odd_lane = jnp.where(keep_lane, -r1 / pivot, 0.0)
            m = m_ref[lo:, lo:]
            window = m[:, :reach]
            col_even = jnp.sum(jnp.where(lanes == first, window, 0.0), axis=1, keepdims=True)
            col_odd = jnp.sum(jnp.where(lanes == first + 1, window, 0.0), axis=1, keepdims=True)
            low_even = col_even[size - lo:]
            low_odd = col_odd[size - lo:]
            scaled = jnp.where(low_lanes == first, low_odd / pivot, scaled)
            scaled = jnp.where(low_lanes == first + 1, -low_even / pivot, scaled)
            pivots = jnp.where(lane_full == k, pivot, pivots)
            keep_row = row_idx > first + 1
            col_even = jnp.where(keep_row, col_even, 0.0)
            col_odd = jnp.where(keep_row, col_odd, 0.0)
            m_ref[lo:, lo:] = m + (col_odd * even_lane - col_even * odd_lane)
            return (pivots, scaled)

        return step

    carry = (jnp.zeros((1, size), jnp.float32), jnp.zeros((below, size), jnp.float32))
    carry = lax.fori_loop(0, half // 2, make_step(0), carry, unroll=2)
    pivots, scaled = lax.fori_loop(half // 2, size // 2, make_step(half), carry, unroll=2)
    pc_ref[...] = m_ref[size:, :]
    piv_ref[...] = pivots
    scaled_ref[...] = scaled


def factor_augmented(block, first, strength_col, below, share):
    width = block.shape[1]
    size = width
    rows = size + below
    vmem = pl.BlockSpec(memory_space=pltpu.VMEM)
    return pl.pallas_call(
        functools.partial(factor_kernel, share),
        out_shape=(
            jax.ShapeDtypeStruct((below, width), jnp.float32),
            jax.ShapeDtypeStruct((1, width), jnp.float32),
            jax.ShapeDtypeStruct((below, width), jnp.float32),
        ),
        in_specs=[vmem, vmem, vmem],
        out_specs=(vmem, vmem, vmem),
        scratch_shapes=[pltpu.VMEM((rows, width), jnp.float32)],
    )(block, first, strength_col)


def gather_rows(x, stages):
    return gather_stages(x, stages)[-1]


def gather_stages(x, stages):
    outs = []
    for axes in stages:
        x = lax.all_gather(x, axes, axis=0, tiled=True)
        outs.append(x)
    return outs


def make_on_device(stages, grp_axes):
    def on_device(feats, perm, w_left, w_right, bias_in, w_hidden, bias_hidden, w_out, pair_strength):
        groups = lax.psum(1, grp_axes)
        device = lax.axis_index(grp_axes)
        electrons = perm.shape[0]
        hid = w_left.shape[1]
        panel = 2 * pair_strength.shape[0]
        share = panel // groups
        tail = (electrons - panel) // groups
        w_both = jnp.concatenate([w_left, w_right], axis=1)
        both_own = jnp.dot(feats, w_both, preferred_element_type=jnp.float32).astype(jnp.bfloat16)
        both_every = gather_rows(both_own, stages)
        width = panel
        lanes = 128

        def columns(rows_both):
            stacked = jnp.stack([rows_both[:, :hid], rows_both[:, hid:]])[..., None]
            return jnp.broadcast_to(stacked, stacked.shape[:-1] + (lanes,))

        def transposed(rows_both):
            return jnp.stack([rows_both[:, hid:].T, rows_both[:, :hid].T])

        params = (
            jnp.broadcast_to(0.5 * bias_in[:, None], (hid, width)),
            (w_hidden.T * 0.5).astype(w_hidden.dtype),
            jnp.broadcast_to(0.5 * bias_hidden[:, None], (hid, width)),
            jnp.broadcast_to(w_out[:, None], (hid, width)),
        )
        top_both = 0.5 * jnp.take(both_every, perm[:panel], axis=0).astype(jnp.float32)
        top_own = lax.dynamic_slice_in_dim(top_both, device * share, share, 0)
        top_rows = orbital_rows(columns(top_own), transposed(top_both), params, 0, 1, width)
        pad = (-share) % 8
        top_padded = jnp.pad(top_rows, ((0, pad), (0, 0)))
        partial = gather_stages(top_padded, stages)
        gathered = partial[-1]
        late_every, _ = lax.optimization_barrier((both_every, partial[0]))
        halves = 0.5 * jnp.take(late_every, perm, axis=0).astype(jnp.float32)
        mats = transposed(halves)
        tail_own = lax.dynamic_slice_in_dim(halves, panel + device * tail, tail, 0)
        tail_cols = columns(tail_own)
        blocks = electrons // width
        early = 1
        first_part = orbital_rows(tail_cols, mats, params, 0, 1 + early, width)
        trailing_a = first_part[:, panel:]
        extra = (-tail) % 8
        strength_col = jnp.repeat(pair_strength, 2)[:, None]
        pc, piv_row, scaled = factor_augmented(gathered, first_part, strength_col, tail + extra, share)
        pivots = piv_row[0, : panel // 2]
        log_pivot = jnp.log(jnp.abs(pivots))
        panel_own = pc[:tail]
        scaled_own = scaled[:tail]
        scaled_all = gather_rows(scaled_own, stages)
        trailing_b = orbital_rows(
            tail_cols, mats, params, 1 + early, blocks - 1 - early, width, after=piv_row
        )
        trailing_own = jnp.concatenate([trailing_a, trailing_b], axis=1)
        schur = trailing_own - jnp.dot(
            panel_own,
            scaled_all.T,
            precision=lax.Precision.HIGHEST,
        )
        return (log_pivot, panel_own, schur)

    return on_device


def split_grp(mesh):
    devs = mesh.devices
    try:
        coords = np.array([[d.coords[2], d.coords[0], d.coords[1]] for d in devs[0]])
        sizes = tuple(len(np.unique(coords[:, i])) for i in range(3))
        grid = coords.reshape(sizes + (3,))
        ok = int(np.prod(sizes)) == devs.shape[1]
        for i in range(3):
            idx = np.arange(sizes[i]).reshape([-1 if j == i else 1 for j in range(3)])
            ok = ok and bool(np.all(grid[..., i] == idx))
    except Exception:
        ok = False
    if not ok:
        return None
    return Mesh(devs.reshape((devs.shape[0],) + sizes), ("walker", "z", "x", "y"))


def solution(mesh):
    split = split_grp(mesh)
    if split is None:
        use, grp_axes, stages = mesh, "grp", ("grp",)
    else:
        use, grp_axes, stages = split, ("z", "x", "y"), (("x", "y"), "z")
    rows = ("walker",) + ((grp_axes,) if isinstance(grp_axes, str) else grp_axes)
    return jax.shard_map(
        make_on_device(stages, grp_axes),
        mesh=use,
        in_specs=(P(rows, None), P("walker"), P(), P(), P(), P(), P(), P(), P()),
        out_specs=(P("walker"), P(rows, None), P(rows, None)),
        check_vma=False,
    )
```

```python
import functools

import numpy as np
import jax
import jax.numpy as jnp
from jax import lax
from jax.experimental import pallas as pl
from jax.experimental.pallas import tpu as pltpu
from jax.sharding import Mesh
from jax.sharding import PartitionSpec as P


def orbital_kernel(col_ref, mat_ref, bias_in_ref, w_hid_t_ref, bias_hid_ref, w_out_ref, *rest):
    out_ref = rest[-1]
    rows = col_ref.shape[1]
    copies = mat_ref.shape[2] // col_ref.shape[3]
    w_hid_t = w_hid_t_ref[...]

    def one(d, r):
        col = col_ref[d, r]
        col = jnp.concatenate([col] * copies, axis=1) if copies > 1 else col
        half = (col + mat_ref[d]) + bias_in_ref[...]
        gated = (half * (1.0 + jnp.tanh(half))).astype(jnp.bfloat16)
        half = jnp.dot(w_hid_t, gated, preferred_element_type=jnp.float32) + bias_hid_ref[...]
        return jnp.sum(half * (1.0 + jnp.tanh(half)) * w_out_ref[...], axis=0, keepdims=True)

    def body(r, carry):
        out_ref[pl.ds(r, 1), :] = one(0, r) - one(1, r)
        return carry

    lax.fori_loop(0, rows, body, 0)


def orbital_rows(cols, mats, params, first, blocks, width, after=None):
    _, rows, feat, lanes = cols.shape
    count = blocks * width
    flops = 2 * rows * count * (2 * feat * feat + 12 * feat)
    operands = [cols, mats, *params]
    in_specs = [
        pl.BlockSpec((2, rows, feat, lanes), lambda j: (0, 0, 0, 0)),
        pl.BlockSpec((2, feat, width), lambda j: (0, 0, j + first)),
        pl.BlockSpec((feat, width), lambda j: (0, 0)),
        pl.BlockSpec((feat, feat), lambda j: (0, 0)),
        pl.BlockSpec((feat, width), lambda j: (0, 0)),
        pl.BlockSpec((feat, width), lambda j: (0, 0)),
    ]
    if after is not None:
        operands.append(after)
        in_specs.append(pl.BlockSpec(after.shape, lambda j: (0, 0)))
    return pl.pallas_call(
        orbital_kernel,
        grid=(blocks,),
        out_shape=jax.ShapeDtypeStruct((rows, count), jnp.float32),
        in_specs=in_specs,
        out_specs=pl.BlockSpec((rows, width), lambda j: (0, j)),
        cost_estimate=pl.CostEstimate(
            flops=flops,
            transcendentals=4 * rows * count * feat,
            bytes_accessed=4 * (2 * feat * count + rows * count),
        ),
    )(*operands)


def factor_kernel(share, block_ref, first_ref, ps_ref, pc_ref, piv_ref, scaled_ref, m_ref):
    rows, size = m_ref.shape
    half = size // 2
    below = rows - size
    own = first_ref.shape[0]
    lanes_blk = lax.broadcasted_iota(jnp.int32, (size, size), 1)
    row_blk = lax.broadcasted_iota(jnp.int32, (size, 1), 0)
    strength = ps_ref[...]
    stride = block_ref.shape[0] * share // size

    for g in range(size // share):
        m_ref[g * share:(g + 1) * share, :] = block_ref[g * stride:g * stride + share, :]
    m0 = m_ref[:size, :]
    m0 = m0 + jnp.where((row_blk % 2 == 0) & (lanes_blk == row_blk + 1), strength, 0.0)
    m0 = m0 - jnp.where((row_blk % 2 == 1) & (lanes_blk == row_blk - 1), strength, 0.0)
    m_ref[:size, :] = m0
    m_ref[size:, :] = jnp.zeros((below, size), jnp.float32)
    m_ref[size:size + own, :] = first_ref[:, :size]
    lane_full = lax.broadcasted_iota(jnp.int32, (1, size), 1)
    low_lanes = lax.broadcasted_iota(jnp.int32, (below, size), 1)

    def make_step(lo):
        sub_rows, sub_cols = rows - lo, size - lo
        reach = min(half, sub_cols)
        lane = lax.broadcasted_iota(jnp.int32, (1, sub_cols), 1) + lo
        lanes = lax.broadcasted_iota(jnp.int32, (sub_rows, reach), 1) + lo
        row_idx = lax.broadcasted_iota(jnp.int32, (sub_rows, 1), 0) + lo

        def step(k, carry):
            pivots, scaled = carry
            first = 2 * k
            r0 = m_ref[pl.ds(first, 1), :][:, lo:]
            r1 = m_ref[pl.ds(first + 1, 1), :][:, lo:]
            pivot = jnp.sum(jnp.where(lane == first + 1, r0, 0.0), axis=1, keepdims=True)
            keep_lane = lane > first + 1
            even_lane = jnp.where(keep_lane, -r0 / pivot, 0.0)
            odd_lane = jnp.where(keep_lane, -r1 / pivot, 0.0)
            m = m_ref[lo:, lo:]
            window = m[:, :reach]
            col_even = jnp.sum(jnp.where(lanes == first, window, 0.0), axis=1, keepdims=True)
            col_odd = jnp.sum(jnp.where(lanes == first + 1, window, 0.0), axis=1, keepdims=True)
            low_even = col_even[size - lo:]
            low_odd = col_odd[size - lo:]
            scaled = jnp.where(low_lanes == first, low_odd / pivot, scaled)
            scaled = jnp.where(low_lanes == first + 1, -low_even / pivot, scaled)
            pivots = jnp.where(lane_full == k, pivot, pivots)
            keep_row = row_idx > first + 1
            col_even = jnp.where(keep_row, col_even, 0.0)
            col_odd = jnp.where(keep_row, col_odd, 0.0)
            m_ref[lo:, lo:] = m + (col_odd * even_lane - col_even * odd_lane)
            return (pivots, scaled)

        return step

    carry = (jnp.zeros((1, size), jnp.float32), jnp.zeros((below, size), jnp.float32))
    carry = lax.fori_loop(0, half // 2, make_step(0), carry, unroll=2)
    pivots, scaled = lax.fori_loop(half // 2, size // 2, make_step(half), carry, unroll=2)
    pc_ref[...] = m_ref[size:, :]
    piv_ref[...] = pivots
    scaled_ref[...] = scaled


def factor_augmented(block, first, strength_col, below, share):
    width = block.shape[1]
    size = width
    rows = size + below
    vmem = pl.BlockSpec(memory_space=pltpu.VMEM)
    return pl.pallas_call(
        functools.partial(factor_kernel, share),
        out_shape=(
            jax.ShapeDtypeStruct((below, width), jnp.float32),
            jax.ShapeDtypeStruct((1, width), jnp.float32),
            jax.ShapeDtypeStruct((below, width), jnp.float32),
        ),
        in_specs=[vmem, vmem, vmem],
        out_specs=(vmem, vmem, vmem),
        scratch_shapes=[pltpu.VMEM((rows, width), jnp.float32)],
    )(block, first, strength_col)


def gather_rows(x, stages):
    return gather_stages(x, stages)[-1]


def gather_stages(x, stages):
    outs = []
    for axes in stages:
        x = lax.all_gather(x, axes, axis=0, tiled=True)
        outs.append(x)
    return outs


def make_on_device(stages, grp_axes):
    def on_device(feats, perm, w_left, w_right, bias_in, w_hidden, bias_hidden, w_out, pair_strength):
        groups = lax.psum(1, grp_axes)
        device = lax.axis_index(grp_axes)
        electrons = perm.shape[0]
        hid = w_left.shape[1]
        panel = 2 * pair_strength.shape[0]
        share = panel // groups
        tail = (electrons - panel) // groups
        w_both = jnp.concatenate([w_left, w_right], axis=1)
        both_own = jnp.dot(feats, w_both, preferred_element_type=jnp.float32).astype(jnp.bfloat16)
        lr_partial = gather_stages(both_own, stages)
        both_every = lr_partial[-1]
        width = panel
        lanes = 128

        def columns(rows_both):
            stacked = jnp.stack([rows_both[:, :hid], rows_both[:, hid:]])[..., None]
            return jnp.broadcast_to(stacked, stacked.shape[:-1] + (lanes,))

        def transposed(rows_both):
            return jnp.stack([rows_both[:, hid:].T, rows_both[:, :hid].T])

        params = (
            jnp.broadcast_to(0.5 * bias_in[:, None], (hid, width)),
            (w_hidden.T * 0.5).astype(w_hidden.dtype),
            jnp.broadcast_to(0.5 * bias_hidden[:, None], (hid, width)),
            jnp.broadcast_to(w_out[:, None], (hid, width)),
        )
        _, params = lax.optimization_barrier((lr_partial[0], params))
        top_both = 0.5 * jnp.take(both_every, perm[:panel], axis=0).astype(jnp.float32)
        top_own = lax.dynamic_slice_in_dim(top_both, device * share, share, 0)
        top_rows = orbital_rows(columns(top_own), transposed(top_both), params, 0, 1, width)
        pad = (-share) % 8
        top_padded = jnp.pad(top_rows, ((0, pad), (0, 0)))
        partial = gather_stages(top_padded, stages)
        gathered = partial[-1]
        late_every, _ = lax.optimization_barrier((both_every, partial[0]))
        halves = 0.5 * jnp.take(late_every, perm, axis=0).astype(jnp.float32)
        mats = transposed(halves)
        tail_own = lax.dynamic_slice_in_dim(halves, panel + device * tail, tail, 0)
        tail_cols = columns(tail_own)
        blocks = electrons // width
        early = 1
        first_part = orbital_rows(tail_cols, mats, params, 0, 1 + early, width)
        trailing_a = first_part[:, panel:]
        extra = (-tail) % 8
        strength_col = jnp.repeat(pair_strength, 2)[:, None]
        pc, piv_row, scaled = factor_augmented(gathered, first_part, strength_col, tail + extra, share)
        pivots = piv_row[0, : panel // 2]
        log_pivot = jnp.log(jnp.abs(pivots))
        panel_own = pc[:tail]
        scaled_own = scaled[:tail]
        scaled_all = gather_rows(scaled_own, stages)
        trailing_b = orbital_rows(
            tail_cols, mats, params, 1 + early, blocks - 1 - early, width, after=piv_row
        )
        trailing_own = jnp.concatenate([trailing_a, trailing_b], axis=1)
        schur = trailing_own - jnp.dot(
            panel_own,
            scaled_all.T,
            precision=lax.Precision.HIGHEST,
        )
        return (log_pivot, panel_own, schur)

    return on_device


def split_grp(mesh):
    devs = mesh.devices
    try:
        coords = np.array([[d.coords[2], d.coords[0], d.coords[1]] for d in devs[0]])
        sizes = tuple(len(np.unique(coords[:, i])) for i in range(3))
        grid = coords.reshape(sizes + (3,))
        ok = int(np.prod(sizes)) == devs.shape[1]
        for i in range(3):
            idx = np.arange(sizes[i]).reshape([-1 if j == i else 1 for j in range(3)])
            ok = ok and bool(np.all(grid[..., i] == idx))
    except Exception:
        ok = False
    if not ok:
        return None
    return Mesh(devs.reshape((devs.shape[0],) + sizes), ("walker", "z", "x", "y"))


def solution(mesh):
    split = split_grp(mesh)
    if split is None:
        use, grp_axes, stages = mesh, "grp", ("grp",)
    else:
        use, grp_axes, stages = split, ("z", "x", "y"), (("x", "y"), "z")
    rows = ("walker",) + ((grp_axes,) if isinstance(grp_axes, str) else grp_axes)
    return jax.shard_map(
        make_on_device(stages, grp_axes),
        mesh=use,
        in_specs=(P(rows, None), P("walker"), P(), P(), P(), P(), P(), P(), P()),
        out_specs=(P("walker"), P(rows, None), P(rows, None)),
        check_vma=False,
    )
```

```python
import functools

import numpy as np
import jax
import jax.numpy as jnp
from jax import lax
from jax.experimental import pallas as pl
from jax.experimental.pallas import tpu as pltpu
from jax.sharding import Mesh
from jax.sharding import PartitionSpec as P


def orbital_kernel(col_ref, mat_ref, bias_in_ref, w_hid_t_ref, bias_hid_ref, w_out_ref, *rest):
    out_ref = rest[-1]
    rows = col_ref.shape[1]
    copies = mat_ref.shape[2] // col_ref.shape[3]
    w_hid_t = w_hid_t_ref[...]

    def one(d, r):
        col = col_ref[d, r]
        col = jnp.concatenate([col] * copies, axis=1) if copies > 1 else col
        half = (col + mat_ref[d]) + bias_in_ref[...]
        gated = (half * (1.0 + jnp.tanh(half))).astype(jnp.bfloat16)
        half = jnp.dot(w_hid_t, gated, preferred_element_type=jnp.float32) + bias_hid_ref[...]
        return jnp.sum(half * (1.0 + jnp.tanh(half)) * w_out_ref[...], axis=0, keepdims=True)

    def body(r, carry):
        out_ref[pl.ds(r, 1), :] = one(0, r) - one(1, r)
        return carry

    lax.fori_loop(0, rows, body, 0)


def orbital_rows(cols, mats, params, first, blocks, width, after=None):
    _, rows, feat, lanes = cols.shape
    count = blocks * width
    flops = 2 * rows * count * (2 * feat * feat + 12 * feat)
    operands = [cols, mats, *params]
    in_specs = [
        pl.BlockSpec((2, rows, feat, lanes), lambda j: (0, 0, 0, 0)),
        pl.BlockSpec((2, feat, width), lambda j: (0, 0, j + first)),
        pl.BlockSpec((feat, width), lambda j: (0, 0)),
        pl.BlockSpec((feat, feat), lambda j: (0, 0)),
        pl.BlockSpec((feat, width), lambda j: (0, 0)),
        pl.BlockSpec((feat, width), lambda j: (0, 0)),
    ]
    if after is not None:
        operands.append(after)
        in_specs.append(pl.BlockSpec(after.shape, lambda j: (0, 0)))
    return pl.pallas_call(
        orbital_kernel,
        grid=(blocks,),
        out_shape=jax.ShapeDtypeStruct((rows, count), jnp.float32),
        in_specs=in_specs,
        out_specs=pl.BlockSpec((rows, width), lambda j: (0, j)),
        cost_estimate=pl.CostEstimate(
            flops=flops,
            transcendentals=4 * rows * count * feat,
            bytes_accessed=4 * (2 * feat * count + rows * count),
        ),
    )(*operands)


def factor_kernel(share, block_ref, first_ref, ps_ref, pc_ref, piv_ref, scaled_ref, m_ref):
    rows, size = m_ref.shape
    half = size // 2
    below = rows - size
    own = first_ref.shape[0]
    lanes_blk = lax.broadcasted_iota(jnp.int32, (size, size), 1)
    row_blk = lax.broadcasted_iota(jnp.int32, (size, 1), 0)
    strength = ps_ref[...]
    stride = block_ref.shape[0] * share // size

    for g in range(size // share):
        m_ref[g * share:(g + 1) * share, :] = block_ref[g * stride:g * stride + share, :]
    m0 = m_ref[:size, :]
    m0 = m0 + jnp.where((row_blk % 2 == 0) & (lanes_blk == row_blk + 1), strength, 0.0)
    m0 = m0 - jnp.where((row_blk % 2 == 1) & (lanes_blk == row_blk - 1), strength, 0.0)
    m_ref[:size, :] = m0
    m_ref[size:, :] = jnp.zeros((below, size), jnp.float32)
    m_ref[size:size + own, :] = first_ref[:, :size]
    lane_full = lax.broadcasted_iota(jnp.int32, (1, size), 1)
    low_lanes = lax.broadcasted_iota(jnp.int32, (below, size), 1)

    def make_step(lo):
        sub_rows, sub_cols = rows - lo, size - lo
        reach = min(half, sub_cols)
        lane = lax.broadcasted_iota(jnp.int32, (1, sub_cols), 1) + lo
        lanes = lax.broadcasted_iota(jnp.int32, (sub_rows, reach), 1) + lo
        row_idx = lax.broadcasted_iota(jnp.int32, (sub_rows, 1), 0) + lo

        def step(k, carry):
            pivots, scaled = carry
            first = 2 * k
            r0 = m_ref[pl.ds(first, 1), :][:, lo:]
            r1 = m_ref[pl.ds(first + 1, 1), :][:, lo:]
            pivot = jnp.sum(jnp.where(lane == first + 1, r0, 0.0), axis=1, keepdims=True)
            keep_lane = lane > first + 1
            even_lane = jnp.where(keep_lane, -r0 / pivot, 0.0)
            odd_lane = jnp.where(keep_lane, -r1 / pivot, 0.0)
            m = m_ref[lo:, lo:]
            window = m[:, :reach]
            col_even = jnp.sum(jnp.where(lanes == first, window, 0.0), axis=1, keepdims=True)
            col_odd = jnp.sum(jnp.where(lanes == first + 1, window, 0.0), axis=1, keepdims=True)
            low_even = col_even[size - lo:]
            low_odd = col_odd[size - lo:]
            scaled = jnp.where(low_lanes == first, low_odd / pivot, scaled)
            scaled = jnp.where(low_lanes == first + 1, -low_even / pivot, scaled)
            pivots = jnp.where(lane_full == k, pivot, pivots)
            keep_row = row_idx > first + 1
            col_even = jnp.where(keep_row, col_even, 0.0)
            col_odd = jnp.where(keep_row, col_odd, 0.0)
            m_ref[lo:, lo:] = m + (col_odd * even_lane - col_even * odd_lane)
            return (pivots, scaled)

        return step

    carry = (jnp.zeros((1, size), jnp.float32), jnp.zeros((below, size), jnp.float32))
    carry = lax.fori_loop(0, half // 2, make_step(0), carry, unroll=2)
    pivots, scaled = lax.fori_loop(half // 2, size // 2, make_step(half), carry, unroll=2)
    pc_ref[...] = m_ref[size:, :]
    piv_ref[...] = pivots
    scaled_ref[...] = scaled


def factor_augmented(block, first, strength_col, below, share):
    width = block.shape[1]
    size = width
    rows = size + below
    vmem = pl.BlockSpec(memory_space=pltpu.VMEM)
    return pl.pallas_call(
        functools.partial(factor_kernel, share),
        out_shape=(
            jax.ShapeDtypeStruct((below, width), jnp.float32),
            jax.ShapeDtypeStruct((1, width), jnp.float32),
            jax.ShapeDtypeStruct((below, width), jnp.float32),
        ),
        in_specs=[vmem, vmem, vmem],
        out_specs=(vmem, vmem, vmem),
        scratch_shapes=[pltpu.VMEM((rows, width), jnp.float32)],
    )(block, first, strength_col)


def gather_rows(x, stages):
    return gather_stages(x, stages)[-1]


def gather_stages(x, stages):
    outs = []
    for axes in stages:
        x = lax.all_gather(x, axes, axis=0, tiled=True)
        outs.append(x)
    return outs


def make_on_device(stages, grp_axes):
    def on_device(feats, perm, w_left, w_right, bias_in, w_hidden, bias_hidden, w_out, pair_strength):
        groups = lax.psum(1, grp_axes)
        device = lax.axis_index(grp_axes)
        electrons = perm.shape[0]
        hid = w_left.shape[1]
        panel = 2 * pair_strength.shape[0]
        share = panel // groups
        tail = (electrons - panel) // groups
        w_both = jnp.concatenate([w_left, w_right], axis=1)
        both_own = jnp.dot(feats, w_both, preferred_element_type=jnp.float32).astype(jnp.bfloat16)
        lr_partial = gather_stages(both_own, stages)
        both_every = lr_partial[-1]
        width = panel
        lanes = 128

        def columns(rows_both):
            stacked = jnp.stack([rows_both[:, :hid], rows_both[:, hid:]])[..., None]
            return jnp.broadcast_to(stacked, stacked.shape[:-1] + (lanes,))

        def transposed(rows_both):
            return jnp.stack([rows_both[:, hid:].T, rows_both[:, :hid].T])

        params = (
            jnp.broadcast_to(0.5 * bias_in[:, None], (hid, width)),
            (w_hidden.T * 0.5).astype(w_hidden.dtype),
            jnp.broadcast_to(0.5 * bias_hidden[:, None], (hid, width)),
            jnp.broadcast_to(w_out[:, None], (hid, width)),
        )
        _, params = lax.optimization_barrier((lr_partial[0], params))
        selector = jnp.where(
            jnp.arange(electrons, dtype=perm.dtype)[None, :] == perm[:panel, None], 0.5, 0.0
        ).astype(jnp.bfloat16)
        top_both = jnp.dot(selector, both_every, preferred_element_type=jnp.float32)
        top_own = lax.dynamic_slice_in_dim(top_both, device * share, share, 0)
        top_rows = orbital_rows(columns(top_own), transposed(top_both), params, 0, 1, width)
        pad = (-share) % 8
        top_padded = jnp.pad(top_rows, ((0, pad), (0, 0)))
        partial = gather_stages(top_padded, stages)
        gathered = partial[-1]
        late_every, _ = lax.optimization_barrier((both_every, partial[0]))
        halves = 0.5 * jnp.take(late_every, perm, axis=0).astype(jnp.float32)
        mats = transposed(halves)
        tail_own = lax.dynamic_slice_in_dim(halves, panel + device * tail, tail, 0)
        tail_cols = columns(tail_own)
        blocks = electrons // width
        early = 1
        first_part = orbital_rows(tail_cols, mats, params, 0, 1 + early, width)
        trailing_a = first_part[:, panel:]
        extra = (-tail) % 8
        strength_col = jnp.repeat(pair_strength, 2)[:, None]
        pc, piv_row, scaled = factor_augmented(gathered, first_part, strength_col, tail + extra, share)
        pivots = piv_row[0, : panel // 2]
        log_pivot = jnp.log(jnp.abs(pivots))
        panel_own = pc[:tail]
        scaled_own = scaled[:tail]
        scaled_all = gather_rows(scaled_own, stages)
        trailing_b = orbital_rows(
            tail_cols, mats, params, 1 + early, blocks - 1 - early, width, after=piv_row
        )
        trailing_own = jnp.concatenate([trailing_a, trailing_b], axis=1)
        schur = trailing_own - jnp.dot(
            panel_own,
            scaled_all.T,
            precision=lax.Precision.HIGHEST,
        )
        return (log_pivot, panel_own, schur)

    return on_device


def split_grp(mesh):
    devs = mesh.devices
    try:
        coords = np.array([[d.coords[2], d.coords[0], d.coords[1]] for d in devs[0]])
        sizes = tuple(len(np.unique(coords[:, i])) for i in range(3))
        grid = coords.reshape(sizes + (3,))
        ok = int(np.prod(sizes)) == devs.shape[1]
        for i in range(3):
            idx = np.arange(sizes[i]).reshape([-1 if j == i else 1 for j in range(3)])
            ok = ok and bool(np.all(grid[..., i] == idx))
    except Exception:
        ok = False
    if not ok:
        return None
    return Mesh(devs.reshape((devs.shape[0],) + sizes), ("walker", "z", "x", "y"))


def solution(mesh):
    split = split_grp(mesh)
    if split is None:
        use, grp_axes, stages = mesh, "grp", ("grp",)
    else:
        use, grp_axes, stages = split, ("z", "x", "y"), (("x", "y"), "z")
    rows = ("walker",) + ((grp_axes,) if isinstance(grp_axes, str) else grp_axes)
    return jax.shard_map(
        make_on_device(stages, grp_axes),
        mesh=use,
        in_specs=(P(rows, None), P("walker"), P(), P(), P(), P(), P(), P(), P()),
        out_specs=(P("walker"), P(rows, None), P(rows, None)),
        check_vma=False,
    )
```

```python
import functools

import numpy as np
import jax
import jax.numpy as jnp
from jax import lax
from jax.experimental import pallas as pl
from jax.experimental.pallas import tpu as pltpu
from jax.sharding import Mesh
from jax.sharding import PartitionSpec as P


def orbital_kernel(col_ref, mat_ref, bias_in_ref, w_hid_t_ref, bias_hid_ref, w_out_ref, *rest):
    out_ref = rest[-1]
    rows = col_ref.shape[1]
    copies = mat_ref.shape[2] // col_ref.shape[3]
    w_hid_t = w_hid_t_ref[...]

    def one(d, r):
        col = col_ref[d, r]
        col = jnp.concatenate([col] * copies, axis=1) if copies > 1 else col
        half = (col + mat_ref[d]) + bias_in_ref[...]
        gated = (half * (1.0 + jnp.tanh(half))).astype(jnp.bfloat16)
        half = jnp.dot(w_hid_t, gated, preferred_element_type=jnp.float32) + bias_hid_ref[...]
        return jnp.sum(half * (1.0 + jnp.tanh(half)) * w_out_ref[...], axis=0, keepdims=True)

    def body(r, carry):
        out_ref[pl.ds(r, 1), :] = one(0, r) - one(1, r)
        return carry

    if out_ref.shape[0] > rows:
        out_ref[...] = jnp.zeros(out_ref.shape, out_ref.dtype)
    lax.fori_loop(0, rows, body, 0)


def orbital_rows(cols, mats, params, first, blocks, width, after=None, out_rows=None):
    _, rows, feat, lanes = cols.shape
    out_rows = rows if out_rows is None else out_rows
    count = blocks * width
    flops = 2 * rows * count * (2 * feat * feat + 12 * feat)
    operands = [cols, mats, *params]
    in_specs = [
        pl.BlockSpec((2, rows, feat, lanes), lambda j: (0, 0, 0, 0)),
        pl.BlockSpec((2, feat, width), lambda j: (0, 0, j + first)),
        pl.BlockSpec((feat, width), lambda j: (0, 0)),
        pl.BlockSpec((feat, feat), lambda j: (0, 0)),
        pl.BlockSpec((feat, width), lambda j: (0, 0)),
        pl.BlockSpec((feat, width), lambda j: (0, 0)),
    ]
    if after is not None:
        operands.append(after)
        in_specs.append(pl.BlockSpec(after.shape, lambda j: (0, 0)))
    return pl.pallas_call(
        orbital_kernel,
        grid=(blocks,),
        out_shape=jax.ShapeDtypeStruct((out_rows, count), jnp.float32),
        in_specs=in_specs,
        out_specs=pl.BlockSpec((out_rows, width), lambda j: (0, j)),
        cost_estimate=pl.CostEstimate(
            flops=flops,
            transcendentals=4 * rows * count * feat,
            bytes_accessed=4 * (2 * feat * count + rows * count),
        ),
    )(*operands)


def factor_kernel(share, block_ref, first_ref, ps_ref, pc_ref, piv_ref, scaled_ref, m_ref):
    rows, size = m_ref.shape
    half = size // 2
    below = rows - size
    own = first_ref.shape[0]
    lanes_blk = lax.broadcasted_iota(jnp.int32, (size, size), 1)
    row_blk = lax.broadcasted_iota(jnp.int32, (size, 1), 0)
    strength = ps_ref[...]
    stride = block_ref.shape[0] * share // size

    for g in range(size // share):
        m_ref[g * share:(g + 1) * share, :] = block_ref[g * stride:g * stride + share, :]
    m0 = m_ref[:size, :]
    m0 = m0 + jnp.where((row_blk % 2 == 0) & (lanes_blk == row_blk + 1), strength, 0.0)
    m0 = m0 - jnp.where((row_blk % 2 == 1) & (lanes_blk == row_blk - 1), strength, 0.0)
    m_ref[:size, :] = m0
    m_ref[size:, :] = jnp.zeros((below, size), jnp.float32)
    m_ref[size:size + own, :] = first_ref[:, :size]
    lane_full = lax.broadcasted_iota(jnp.int32, (1, size), 1)
    low_lanes = lax.broadcasted_iota(jnp.int32, (below, size), 1)

    def make_step(lo):
        sub_rows, sub_cols = rows - lo, size - lo
        reach = min(half, sub_cols)
        lane = lax.broadcasted_iota(jnp.int32, (1, sub_cols), 1) + lo
        lanes = lax.broadcasted_iota(jnp.int32, (sub_rows, reach), 1) + lo
        row_idx = lax.broadcasted_iota(jnp.int32, (sub_rows, 1), 0) + lo

        def step(k, carry):
            pivots, scaled = carry
            first = 2 * k
            r0 = m_ref[pl.ds(first, 1), :][:, lo:]
            r1 = m_ref[pl.ds(first + 1, 1), :][:, lo:]
            pivot = jnp.sum(jnp.where(lane == first + 1, r0, 0.0), axis=1, keepdims=True)
            keep_lane = lane > first + 1
            even_lane = jnp.where(keep_lane, -r0 / pivot, 0.0)
            odd_lane = jnp.where(keep_lane, -r1 / pivot, 0.0)
            m = m_ref[lo:, lo:]
            window = m[:, :reach]
            col_even = jnp.sum(jnp.where(lanes == first, window, 0.0), axis=1, keepdims=True)
            col_odd = jnp.sum(jnp.where(lanes == first + 1, window, 0.0), axis=1, keepdims=True)
            low_even = col_even[size - lo:]
            low_odd = col_odd[size - lo:]
            scaled = jnp.where(low_lanes == first, low_odd / pivot, scaled)
            scaled = jnp.where(low_lanes == first + 1, -low_even / pivot, scaled)
            pivots = jnp.where(lane_full == k, pivot, pivots)
            keep_row = row_idx > first + 1
            col_even = jnp.where(keep_row, col_even, 0.0)
            col_odd = jnp.where(keep_row, col_odd, 0.0)
            m_ref[lo:, lo:] = m + (col_odd * even_lane - col_even * odd_lane)
            return (pivots, scaled)

        return step

    carry = (jnp.zeros((1, size), jnp.float32), jnp.zeros((below, size), jnp.float32))
    carry = lax.fori_loop(0, half // 2, make_step(0), carry, unroll=4)
    pivots, scaled = lax.fori_loop(half // 2, size // 2, make_step(half), carry, unroll=4)
    pc_ref[...] = m_ref[size:, :]
    piv_ref[...] = pivots
    scaled_ref[...] = scaled


def factor_augmented(block, first, strength_col, below, share):
    width = block.shape[1]
    size = width
    rows = size + below
    vmem = pl.BlockSpec(memory_space=pltpu.VMEM)
    return pl.pallas_call(
        functools.partial(factor_kernel, share),
        out_shape=(
            jax.ShapeDtypeStruct((below, width), jnp.float32),
            jax.ShapeDtypeStruct((1, width), jnp.float32),
            jax.ShapeDtypeStruct((below, width), jnp.float32),
        ),
        in_specs=[vmem, vmem, vmem],
        out_specs=(vmem, vmem, vmem),
        scratch_shapes=[pltpu.VMEM((rows, width), jnp.float32)],
    )(block, first, strength_col)


def gather_rows(x, stages):
    return gather_stages(x, stages)[-1]


def gather_stages(x, stages):
    outs = []
    for axes in stages:
        x = lax.all_gather(x, axes, axis=0, tiled=True)
        outs.append(x)
    return outs


def make_on_device(stages, grp_axes):
    def on_device(feats, perm, w_left, w_right, bias_in, w_hidden, bias_hidden, w_out, pair_strength):
        groups = lax.psum(1, grp_axes)
        device = lax.axis_index(grp_axes)
        electrons = perm.shape[0]
        hid = w_left.shape[1]
        panel = 2 * pair_strength.shape[0]
        share = panel // groups
        tail = (electrons - panel) // groups
        w_both = jnp.concatenate([w_left, w_right], axis=1)
        both_own = jnp.dot(feats, w_both, preferred_element_type=jnp.float32).astype(jnp.bfloat16)
        lr_partial = gather_stages(both_own, stages)
        both_every = lr_partial[-1]
        width = panel
        lanes = 128

        def columns(rows_both):
            stacked = jnp.stack([rows_both[:, :hid], rows_both[:, hid:]])[..., None]
            return jnp.broadcast_to(stacked, stacked.shape[:-1] + (lanes,))

        def transposed(rows_both):
            return jnp.stack([rows_both[:, hid:].T, rows_both[:, :hid].T])

        params = (
            jnp.broadcast_to(0.5 * bias_in[:, None], (hid, width)),
            (w_hidden.T * 0.5).astype(w_hidden.dtype),
            jnp.broadcast_to(0.5 * bias_hidden[:, None], (hid, width)),
            jnp.broadcast_to(w_out[:, None], (hid, width)),
        )
        _, params = lax.optimization_barrier((lr_partial[0], params))
        selector = jnp.where(
            jnp.arange(electrons, dtype=perm.dtype)[None, :] == perm[:panel, None], 0.5, 0.0
        ).astype(jnp.bfloat16)
        top_both = jnp.dot(selector, both_every, preferred_element_type=jnp.float32)
        top_own = lax.dynamic_slice_in_dim(top_both, device * share, share, 0)
        pad = (-share) % 8
        top_padded = orbital_rows(
            columns(top_own), transposed(top_both), params, 0, 1, width, out_rows=share + pad
        )
        partial = gather_stages(top_padded, stages)
        gathered = partial[-1]
        late_every, _ = lax.optimization_barrier((both_every, partial[0]))
        halves = 0.5 * jnp.take(late_every, perm, axis=0).astype(jnp.float32)
        mats = transposed(halves)
        tail_own = lax.dynamic_slice_in_dim(halves, panel + device * tail, tail, 0)
        tail_cols = columns(tail_own)
        blocks = electrons // width
        early = 1
        first_part = orbital_rows(tail_cols, mats, params, 0, 1 + early, width)
        trailing_a = first_part[:, panel:]
        extra = (-tail) % 8
        strength_col = jnp.repeat(pair_strength, 2)[:, None]
        pc, piv_row, scaled = factor_augmented(gathered, first_part, strength_col, tail + extra, share)
        pivots = piv_row[0, : panel // 2]
        log_pivot = jnp.log(jnp.abs(pivots))
        panel_own = pc[:tail]
        scaled_own = scaled[:tail]
        scaled_all = gather_rows(scaled_own, stages)
        trailing_b = orbital_rows(
            tail_cols, mats, params, 1 + early, blocks - 1 - early, width, after=piv_row
        )
        trailing_own = jnp.concatenate([trailing_a, trailing_b], axis=1)
        schur = trailing_own - jnp.dot(
            panel_own,
            scaled_all.T,
            precision=lax.Precision.HIGHEST,
        )
        return (log_pivot, panel_own, schur)

    return on_device


def split_grp(mesh):
    devs = mesh.devices
    try:
        coords = np.array([[d.coords[2], d.coords[0], d.coords[1]] for d in devs[0]])
        sizes = tuple(len(np.unique(coords[:, i])) for i in range(3))
        grid = coords.reshape(sizes + (3,))
        ok = int(np.prod(sizes)) == devs.shape[1]
        for i in range(3):
            idx = np.arange(sizes[i]).reshape([-1 if j == i else 1 for j in range(3)])
            ok = ok and bool(np.all(grid[..., i] == idx))
    except Exception:
        ok = False
    if not ok:
        return None
    return Mesh(devs.reshape((devs.shape[0],) + sizes), ("walker", "z", "x", "y"))


def solution(mesh):
    split = split_grp(mesh)
    if split is None:
        use, grp_axes, stages = mesh, "grp", ("grp",)
    else:
        use, grp_axes, stages = split, ("z", "x", "y"), (("x", "y"), "z")
    rows = ("walker",) + ((grp_axes,) if isinstance(grp_axes, str) else grp_axes)
    return jax.shard_map(
        make_on_device(stages, grp_axes),
        mesh=use,
        in_specs=(P(rows, None), P("walker"), P(), P(), P(), P(), P(), P(), P()),
        out_specs=(P("walker"), P(rows, None), P(rows, None)),
        check_vma=False,
    )
```

```python
import functools

import numpy as np
import jax
import jax.numpy as jnp
from jax import lax
from jax.experimental import pallas as pl
from jax.experimental.pallas import tpu as pltpu
from jax.sharding import Mesh
from jax.sharding import PartitionSpec as P


def orbital_kernel(col_ref, mat_ref, bias_in_ref, w_hid_t_ref, bias_hid_ref, w_out_ref, *rest):
    out_ref = rest[-1]
    rows = col_ref.shape[1]
    copies = mat_ref.shape[2] // col_ref.shape[3]
    w_hid_t = w_hid_t_ref[...]

    def one(d, r):
        col = col_ref[d, r]
        if 1 < col.shape[1] < mat_ref.shape[2]:
            col = jnp.concatenate([col] * copies, axis=1)
        half = (col + mat_ref[d]) + bias_in_ref[...]
        gated = (half * (1.0 + jnp.tanh(half))).astype(jnp.bfloat16)
        half = jnp.dot(w_hid_t, gated, preferred_element_type=jnp.float32) + bias_hid_ref[...]
        return jnp.sum(half * (1.0 + jnp.tanh(half)) * w_out_ref[...], axis=0, keepdims=True)

    def body(r, carry):
        out_ref[pl.ds(r, 1), :] = one(0, r) - one(1, r)
        return carry

    lax.fori_loop(0, rows, body, 0)


def orbital_rows(cols, mats, params, first, blocks, width, after=None):
    _, rows, feat, lanes = cols.shape
    count = blocks * width
    flops = 2 * rows * count * (2 * feat * feat + 12 * feat)
    operands = [cols, mats, *params]
    in_specs = [
        pl.BlockSpec((2, rows, feat, lanes), lambda j: (0, 0, 0, 0)),
        pl.BlockSpec((2, feat, width), lambda j: (0, 0, j + first)),
        pl.BlockSpec((feat, width), lambda j: (0, 0)),
        pl.BlockSpec((feat, feat), lambda j: (0, 0)),
        pl.BlockSpec((feat, width), lambda j: (0, 0)),
        pl.BlockSpec((feat, width), lambda j: (0, 0)),
    ]
    if after is not None:
        operands.append(after)
        in_specs.append(pl.BlockSpec(after.shape, lambda j: (0, 0)))
    return pl.pallas_call(
        orbital_kernel,
        grid=(blocks,),
        out_shape=jax.ShapeDtypeStruct((rows, count), jnp.float32),
        in_specs=in_specs,
        out_specs=pl.BlockSpec((rows, width), lambda j: (0, j)),
        cost_estimate=pl.CostEstimate(
            flops=flops,
            transcendentals=4 * rows * count * feat,
            bytes_accessed=4 * (2 * feat * count + rows * count),
        ),
    )(*operands)


def factor_kernel(share, block_ref, first_ref, ps_ref, pc_ref, piv_ref, scaled_ref, m_ref):
    rows, size = m_ref.shape
    half = size // 2
    below = rows - size
    own = first_ref.shape[0]
    lanes_blk = lax.broadcasted_iota(jnp.int32, (size, size), 1)
    row_blk = lax.broadcasted_iota(jnp.int32, (size, 1), 0)
    strength = ps_ref[...]
    stride = block_ref.shape[0] * share // size

    for g in range(size // share):
        m_ref[g * share:(g + 1) * share, :] = block_ref[g * stride:g * stride + share, :]
    m0 = m_ref[:size, :]
    m0 = m0 + jnp.where((row_blk % 2 == 0) & (lanes_blk == row_blk + 1), strength, 0.0)
    m0 = m0 - jnp.where((row_blk % 2 == 1) & (lanes_blk == row_blk - 1), strength, 0.0)
    m_ref[:size, :] = m0
    m_ref[size:, :] = jnp.zeros((below, size), jnp.float32)
    m_ref[size:size + own, :] = first_ref[:, :size]
    lane_full = lax.broadcasted_iota(jnp.int32, (1, size), 1)
    low_lanes = lax.broadcasted_iota(jnp.int32, (below, size), 1)

    def make_step(lo):
        sub_rows, sub_cols = rows - lo, size - lo
        reach = min(half, sub_cols)
        lane = lax.broadcasted_iota(jnp.int32, (1, sub_cols), 1) + lo
        lanes = lax.broadcasted_iota(jnp.int32, (sub_rows, reach), 1) + lo
        row_idx = lax.broadcasted_iota(jnp.int32, (sub_rows, 1), 0) + lo

        def step(k, carry):
            pivots, scaled = carry
            first = 2 * k
            r0 = m_ref[pl.ds(first, 1), :][:, lo:]
            r1 = m_ref[pl.ds(first + 1, 1), :][:, lo:]
            pivot = jnp.sum(jnp.where(lane == first + 1, r0, 0.0), axis=1, keepdims=True)
            keep_lane = lane > first + 1
            even_lane = jnp.where(keep_lane, -r0 / pivot, 0.0)
            odd_lane = jnp.where(keep_lane, -r1 / pivot, 0.0)
            m = m_ref[lo:, lo:]
            window = m[:, :reach]
            col_even = jnp.sum(jnp.where(lanes == first, window, 0.0), axis=1, keepdims=True)
            col_odd = jnp.sum(jnp.where(lanes == first + 1, window, 0.0), axis=1, keepdims=True)
            low_even = col_even[size - lo:]
            low_odd = col_odd[size - lo:]
            scaled = jnp.where(low_lanes == first, low_odd / pivot, scaled)
            scaled = jnp.where(low_lanes == first + 1, -low_even / pivot, scaled)
            pivots = jnp.where(lane_full == k, pivot, pivots)
            keep_row = row_idx > first + 1
            col_even = jnp.where(keep_row, col_even, 0.0)
            col_odd = jnp.where(keep_row, col_odd, 0.0)
            m_ref[lo:, lo:] = m + (col_odd * even_lane - col_even * odd_lane)
            return (pivots, scaled)

        return step

    carry = (jnp.zeros((1, size), jnp.float32), jnp.zeros((below, size), jnp.float32))
    carry = lax.fori_loop(0, half // 2, make_step(0), carry, unroll=2)
    pivots, scaled = lax.fori_loop(half // 2, size // 2, make_step(half), carry, unroll=2)
    pc_ref[...] = m_ref[size:, :]
    piv_ref[...] = pivots
    scaled_ref[...] = scaled


def factor_augmented(block, first, strength_col, below, share):
    width = block.shape[1]
    size = width
    rows = size + below
    vmem = pl.BlockSpec(memory_space=pltpu.VMEM)
    return pl.pallas_call(
        functools.partial(factor_kernel, share),
        out_shape=(
            jax.ShapeDtypeStruct((below, width), jnp.float32),
            jax.ShapeDtypeStruct((1, width), jnp.float32),
            jax.ShapeDtypeStruct((below, width), jnp.float32),
        ),
        in_specs=[vmem, vmem, vmem],
        out_specs=(vmem, vmem, vmem),
        scratch_shapes=[pltpu.VMEM((rows, width), jnp.float32)],
    )(block, first, strength_col)


def gather_rows(x, stages):
    return gather_stages(x, stages)[-1]


def gather_stages(x, stages):
    outs = []
    for axes in stages:
        x = lax.all_gather(x, axes, axis=0, tiled=True)
        outs.append(x)
    return outs


def make_on_device(stages, grp_axes):
    def on_device(feats, perm, w_left, w_right, bias_in, w_hidden, bias_hidden, w_out, pair_strength):
        groups = lax.psum(1, grp_axes)
        device = lax.axis_index(grp_axes)
        electrons = perm.shape[0]
        hid = w_left.shape[1]
        panel = 2 * pair_strength.shape[0]
        share = panel // groups
        tail = (electrons - panel) // groups
        w_both = jnp.concatenate([w_left, w_right], axis=1)
        both_own = jnp.dot(feats, w_both, preferred_element_type=jnp.float32).astype(jnp.bfloat16)
        lr_partial = gather_stages(both_own, stages)
        both_every = lr_partial[-1]
        width = panel
        lanes = 128

        def columns(rows_both, spread=lanes):
            stacked = jnp.stack([rows_both[:, :hid], rows_both[:, hid:]])[..., None]
            return jnp.broadcast_to(stacked, stacked.shape[:-1] + (spread,))

        def transposed(rows_both):
            return jnp.stack([rows_both[:, hid:].T, rows_both[:, :hid].T])

        params = (
            jnp.broadcast_to(0.5 * bias_in[:, None], (hid, width)),
            (w_hidden.T * 0.5).astype(w_hidden.dtype),
            jnp.broadcast_to(0.5 * bias_hidden[:, None], (hid, width)),
            jnp.broadcast_to(w_out[:, None], (hid, width)),
        )
        _, params = lax.optimization_barrier((lr_partial[0], params))
        selector = jnp.where(
            jnp.arange(electrons, dtype=perm.dtype)[None, :] == perm[:panel, None], 0.5, 0.0
        ).astype(jnp.bfloat16)
        top_both = jnp.dot(selector, both_every, preferred_element_type=jnp.float32)
        top_own = lax.dynamic_slice_in_dim(top_both, device * share, share, 0)
        top_rows = orbital_rows(columns(top_own, 1), transposed(top_both), params, 0, 1, width)
        pad = (-share) % 8
        top_padded = jnp.pad(top_rows, ((0, pad), (0, 0)))
        partial = gather_stages(top_padded, stages)
        gathered = partial[-1]
        late_every, _ = lax.optimization_barrier((both_every, partial[0]))
        halves = 0.5 * jnp.take(late_every, perm, axis=0).astype(jnp.float32)
        mats = transposed(halves)
        tail_own = lax.dynamic_slice_in_dim(halves, panel + device * tail, tail, 0)
        tail_cols = columns(tail_own)
        blocks = electrons // width
        early = 1
        first_part = orbital_rows(tail_cols, mats, params, 0, 1 + early, width)
        trailing_a = first_part[:, panel:]
        extra = (-tail) % 8
        strength_col = jnp.repeat(pair_strength, 2)[:, None]
        pc, piv_row, scaled = factor_augmented(gathered, first_part, strength_col, tail + extra, share)
        pivots = piv_row[0, : panel // 2]
        log_pivot = jnp.log(jnp.abs(pivots))
        panel_own = pc[:tail]
        scaled_own = scaled[:tail]
        scaled_all = gather_rows(scaled_own, stages)
        trailing_b = orbital_rows(
            tail_cols, mats, params, 1 + early, blocks - 1 - early, width, after=piv_row
        )
        trailing_own = jnp.concatenate([trailing_a, trailing_b], axis=1)
        schur = trailing_own - jnp.dot(
            panel_own,
            scaled_all.T,
            precision=lax.Precision.HIGHEST,
        )
        return (log_pivot, panel_own, schur)

    return on_device


def split_grp(mesh):
    devs = mesh.devices
    try:
        coords = np.array([[d.coords[2], d.coords[0], d.coords[1]] for d in devs[0]])
        sizes = tuple(len(np.unique(coords[:, i])) for i in range(3))
        grid = coords.reshape(sizes + (3,))
        ok = int(np.prod(sizes)) == devs.shape[1]
        for i in range(3):
            idx = np.arange(sizes[i]).reshape([-1 if j == i else 1 for j in range(3)])
            ok = ok and bool(np.all(grid[..., i] == idx))
    except Exception:
        ok = False
    if not ok:
        return None
    return Mesh(devs.reshape((devs.shape[0],) + sizes), ("walker", "z", "x", "y"))


def solution(mesh):
    split = split_grp(mesh)
    if split is None:
        use, grp_axes, stages = mesh, "grp", ("grp",)
    else:
        use, grp_axes, stages = split, ("z", "x", "y"), (("x", "y"), "z")
    rows = ("walker",) + ((grp_axes,) if isinstance(grp_axes, str) else grp_axes)
    return jax.shard_map(
        make_on_device(stages, grp_axes),
        mesh=use,
        in_specs=(P(rows, None), P("walker"), P(), P(), P(), P(), P(), P(), P()),
        out_specs=(P("walker"), P(rows, None), P(rows, None)),
        check_vma=False,
    )
```
